128 devices in a mesh: db: 32 (over z, y, x_hi), section: 2 (over core), mp: 2 (over x_lo).
Axes of the slice: x: 4 (x_hi: 2, x_lo: 2; x = x_hi * 2 + x_lo), y: 4, z: 4, core: 2. Of those that a mesh axis runs over, the one named last changes fastest.
Arguments:
- hidden_in: bfloat16 [16384, 4096], P('db', 'mp'), may hold values from -24 to 24
- database: bfloat16 [128, 128, 896], P('db'), may hold values from -8.5 to 8.5
- neighbour_ids: int32 [256, 2], replicated, may hold values from 0 to 127, as said below
- enc_gain: float32 [896], replicated, may hold values from 0.1 to 1.9
- enc_up: bfloat16 [896, 2048], P(None, ('section', 'mp')), may hold values from -0.1875 to 0.1875
- enc_down: bfloat16 [2048, 896], P(('section', 'mp')), may hold values from -0.125 to 0.125
- dec_gain: float32 [2, 4096], P('section'), may hold values from 0.1 to 1.9
- w_query: bfloat16 [2, 4096, 2048], P('section', None, 'mp'), may hold values from -0.06328125 to 0.06328125
- w_key: bfloat16 [2, 896, 2048], P('section', None, 'mp'), may hold values from -0.135301004 to 0.135301004
- w_value: bfloat16 [2, 896, 2048], P('section', None, 'mp'), may hold values from -0.1875 to 0.1875
- w_out: bfloat16 [2, 2048, 4096], P('section', 'mp'), may hold values from -0.125 to 0.125
Outputs:
- hidden_out: bfloat16 [16384, 4096], P(('db', 'section'), 'mp')
The draws below stay inside these ranges and needn't reach their ends.
Inputs may be any that keep to these rules, and one draw needn't show every extreme that they name: `neighbour_ids`: block id b is held by db index b // 4. The 16 ids in the rows of one db index name at most 2 blocks of any one holder, and in every draw one holder is named exactly 2 times by every db index.
All inputs are finite; a program needn't handle non-finite values.
Results may differ from the reference program's by a relative error of at most 0.015.
Values may be sent and summed in bfloat16 or wider, within the bound.
No kernel may reach another device: no remote copies, remote signals or barrier semaphores. Data moves between devices by JAX's collectives and lax.ppermute only.
A program may use at most 128 MiB of HBM per device.

```python
import jax
import jax.numpy as jnp
from jax import lax

D = 4096
HEADS = 16
HD = 128
E = 896
EH = 2048
NEIGH = 2
QBLOCK = 64
NBLOCK = 128
DB_DEV = 4
LAYERS = 2
TOKENS = 16384
QB_DB = 8
QBLOCKS = 256
CAP = 2
DB_BLOCKS = 128


def drawn_or_flat(key, array_shape, spread_scale, clip_bound):
    return jnp.clip(jax.random.normal(key, array_shape, jnp.float32), -clip_bound, clip_bound) * spread_scale


def draw_hidden_in(key, part):
    drawn = drawn_or_flat(jax.random.fold_in(key, 1), (TOKENS, D), 1.0, 6.0)
    return drawn.astype(jnp.bfloat16)


def draw_database(key, part):
    drawn = drawn_or_flat(jax.random.fold_in(key, 1), (DB_BLOCKS, NBLOCK, E), 1.0, 6.0)
    return drawn.astype(jnp.bfloat16)


def draw_w_query(key, part):
    drawn = drawn_or_flat(jax.random.fold_in(key, 1), (LAYERS, D, HEADS * HD), D ** (-0.5), 4.0)
    return drawn.astype(jnp.bfloat16)


def draw_w_key(key, part):
    drawn = drawn_or_flat(jax.random.fold_in(key, 1), (LAYERS, E, HEADS * HD), E ** (-0.5), 4.0)
    return drawn.astype(jnp.bfloat16)


def draw_neighbour_ids(key, part):
    holders = QBLOCKS // QB_DB
    request = NEIGH * QB_DB
    slot_count = holders * CAP
    favoured = jax.random.randint(jax.random.fold_in(key, 7), (), 0, holders)

    def one_source(source):
        subkey = jax.random.fold_in(key, source + 100)
        ranking = jax.random.permutation(jax.random.fold_in(subkey, 1), slot_count)
        holder_of = jnp.arange(slot_count) // CAP
        ranking = jnp.where(holder_of == favoured, -1 - jnp.arange(slot_count), ranking)
        ordered = jnp.argsort(ranking, stable=True)[:request]
        ordered = ordered[jax.random.permutation(jax.random.fold_in(subkey, 2), request)]
        owners = ordered // CAP
        within = jax.random.randint(jax.random.fold_in(subkey, 3), (request,), 0, DB_DEV)
        return (owners * DB_DEV + within).astype(jnp.int32)
    id_grid = jax.vmap(one_source)(jnp.arange(holders))
    return id_grid.reshape(QBLOCKS, NEIGH)


def block_levels(stream_key, shape, shards, smallest, top_value):
    gain = 1.0
    for dim, blocks in shards:
        heights = jax.random.uniform(jax.random.fold_in(jax.random.fold_in(stream_key, 6), dim), (blocks,), jnp.float32, smallest / len(shards), top_value / len(shards))
        gain = gain * jnp.repeat(jnp.exp(heights), shape[dim] // blocks).reshape((-1,) + (1,) * (len(shape) - 1 - dim))
    return gain


def gaussian(key, dims, width, most, cuts=(), held_as=jnp.bfloat16):
    level = block_levels(key, dims, cuts, -0.22, 0.18) if cuts else 1.0
    values = jax.random.normal(key, dims, jnp.float32) * width * level
    return jnp.minimum(jnp.maximum(values, -most), most).astype(held_as)


def setup_inputs(seed: int = 0) -> dict:
    arg_keys = jax.random.split(jax.random.key(seed), 12)
    hidden_in = draw_hidden_in(jax.random.fold_in(arg_keys[11], 71), 0)
    database = draw_database(jax.random.fold_in(arg_keys[11], 71), 0)
    neighbour_ids = draw_neighbour_ids(jax.random.fold_in(arg_keys[11], 71), 0)
    enc_gain = jnp.clip(1.0 + 0.18 * jax.random.normal(arg_keys[3], (E,), jnp.float32), 0.1, 1.9)
    enc_up = gaussian(arg_keys[4], (E, EH), E ** -0.5, 0.1875, ((1, 4),))
    enc_down = gaussian(arg_keys[5], (EH, E), EH ** -0.5, 0.125, ((0, 4),))
    dec_gain = jnp.clip(1.0 + 0.18 * jax.random.normal(arg_keys[6], (LAYERS, D), jnp.float32), 0.1, 1.9)
    w_query = draw_w_query(jax.random.fold_in(arg_keys[11], 71), 0)
    w_key = draw_w_key(jax.random.fold_in(arg_keys[11], 71), 0)
    w_value = gaussian(arg_keys[9], (LAYERS, E, HEADS * HD), E ** -0.5, 0.1875, ((0, 2), (2, 2)))
    w_out = gaussian(arg_keys[10], (LAYERS, HEADS * HD, D), (HEADS * HD) ** -0.5, 0.125, ((0, 2), (1, 2)))
    return dict(hidden_in=hidden_in, database=database, neighbour_ids=neighbour_ids, enc_gain=enc_gain, enc_up=enc_up, enc_down=enc_down, dec_gain=dec_gain, w_query=w_query, w_key=w_key, w_value=w_value, w_out=w_out)


def rms_scale(rows_in, gain_vec):
    return rows_in * lax.rsqrt(lax.optimization_barrier(jnp.mean(rows_in * rows_in, axis=-1, keepdims=True)) + 1e-06) * gain_vec

def encode_rows(rows_in, enc_gain, enc_up, enc_down):
    floats = rows_in.astype(jnp.float32)
    normed = rms_scale(floats, enc_gain).astype(jnp.bfloat16)
    inner_act = jax.nn.gelu(jnp.dot(normed, enc_up, preferred_element_type=jnp.float32), approximate=True).astype(jnp.bfloat16)
    return (floats + jnp.dot(inner_act, enc_down, preferred_element_type=jnp.float32)).astype(jnp.bfloat16)

def cross_layer(state_rows, blocks, gain_vec, query_w, key_w, value_w, out_w):
    floats = state_rows.astype(jnp.float32)
    normed = rms_scale(floats, gain_vec).astype(jnp.bfloat16)
    queries = (jnp.dot(normed, query_w, preferred_element_type=jnp.float32) * HD ** (-0.5)).astype(jnp.bfloat16)
    groups = QBLOCKS // QB_DB
    query_groups = queries.reshape(groups, QB_DB, QBLOCK, HEADS * HD)
    block_groups = blocks.reshape(groups, QB_DB, NEIGH * NBLOCK, E)

    def attend(group_pair):
        query_part, block_part = group_pair
        flat_rows = block_part.reshape(-1, E)
        key_rows = jnp.dot(flat_rows, key_w, preferred_element_type=jnp.float32).astype(jnp.bfloat16)
        value_rows = jnp.dot(flat_rows, value_w, preferred_element_type=jnp.float32).astype(jnp.bfloat16)
        query_four = query_part.reshape(QB_DB, QBLOCK, HEADS, HD).astype(jnp.float32)
        key_four = key_rows.reshape(QB_DB, NEIGH * NBLOCK, HEADS, HD).astype(jnp.float32)
        value_four = value_rows.reshape(QB_DB, NEIGH * NBLOCK, HEADS, HD).astype(jnp.float32)
        scores = jnp.einsum('cqhd,ckhd->chqk', query_four, key_four)
        soft_weights = jax.nn.softmax(scores, axis=-1).astype(jnp.bfloat16)
        context = jnp.einsum('chqk,ckhd->cqhd', soft_weights.astype(jnp.float32), value_four)
        return context.astype(jnp.bfloat16).reshape(QB_DB * QBLOCK, HEADS * HD)
    context = lax.map(attend, (query_groups, block_groups)).reshape(TOKENS, HEADS * HD)
    return (floats + jnp.dot(context, out_w, preferred_element_type=jnp.float32)).astype(jnp.bfloat16)

def reference(hidden_in, database, neighbour_ids, enc_gain, enc_up, enc_down, dec_gain, w_query, w_key, w_value, w_out):
    fetched = database[neighbour_ids.reshape(-1)]
    encoded = encode_rows(fetched.reshape(-1, E), enc_gain, enc_up, enc_down)
    encoded = encoded.reshape(QBLOCKS, NEIGH * NBLOCK, E)
    state_rows = hidden_in
    for layer_id in range(LAYERS):
        state_rows = cross_layer(state_rows, encoded, dec_gain[layer_id], w_query[layer_id], w_key[layer_id], w_value[layer_id], w_out[layer_id])
    return state_rows
```

```python
import jax
import jax.numpy as jnp
from jax import lax
from jax.sharding import PartitionSpec as P

HD = 128
E = 896
NEIGH = 2
QBLOCK = 64
NBLOCK = 128


def rms_scale(rows_in, gain_vec):
    return (
        rows_in * lax.rsqrt(jnp.mean(rows_in * rows_in, axis=-1, keepdims=True) + 1e-06) * gain_vec
    )


def encoder_terms(floats, enc_gain, enc_up, enc_down):
    normed = rms_scale(floats, enc_gain).astype(jnp.bfloat16)
    inner_act = jax.nn.gelu(
        jnp.dot(normed, enc_up, preferred_element_type=jnp.float32), approximate=True
    ).astype(jnp.bfloat16)
    return jnp.dot(inner_act, enc_down, preferred_element_type=jnp.float32)


def cross_layer(state_rows, blocks, gain_vec, query_w, key_w, value_w, out_w):
    block_count = blocks.shape[0]
    whole_rows = lax.all_gather(state_rows, "mp", axis=1, tiled=True)
    floats = whole_rows.astype(jnp.float32)
    normed = rms_scale(floats, gain_vec).astype(jnp.bfloat16)
    queries = (jnp.dot(normed, query_w, preferred_element_type=jnp.float32) * HD ** (-0.5)).astype(
        jnp.bfloat16
    )
    flat_rows = blocks.reshape(-1, E)
    key_rows = jnp.dot(flat_rows, key_w, preferred_element_type=jnp.float32).astype(jnp.bfloat16)
    value_rows = jnp.dot(flat_rows, value_w, preferred_element_type=jnp.float32).astype(
        jnp.bfloat16
    )
    head_count = query_w.shape[1] // HD
    query_four = queries.reshape(block_count, QBLOCK, head_count, HD)
    key_four = key_rows.reshape(block_count, NEIGH * NBLOCK, head_count, HD)
    value_four = value_rows.reshape(block_count, NEIGH * NBLOCK, head_count, HD)
    scores = jnp.einsum("cqhd,ckhd->chqk", query_four, key_four, preferred_element_type=jnp.float32)
    soft_weights = jax.nn.softmax(scores, axis=-1).astype(jnp.bfloat16)
    context = jnp.einsum(
        "chqk,ckhd->cqhd", soft_weights, value_four, preferred_element_type=jnp.float32
    )
    context = context.astype(jnp.bfloat16).reshape(block_count * QBLOCK, head_count * HD)
    partial_out = jnp.dot(context, out_w, preferred_element_type=jnp.float32)
    head_share = lax.psum_scatter(partial_out, "mp", scatter_dimension=1, tiled=True)
    return (state_rows.astype(jnp.float32) + head_share).astype(jnp.bfloat16)


def body(
    hidden_in,
    database,
    neighbour_ids,
    enc_gain,
    enc_up,
    enc_down,
    dec_gain,
    w_query,
    w_key,
    w_value,
    w_out,
):
    db_count = lax.axis_size("db")
    db_index = lax.axis_index("db")
    channels = lax.axis_size("section")
    sec_index = lax.axis_index("section")
    halves = lax.axis_size("mp")
    mp_index = lax.axis_index("mp")
    blocks_held = database.shape[0]
    request = neighbour_ids.shape[0] // db_count * NEIGH
    per_channel = request // channels
    half_rows = NBLOCK // halves
    quarter = half_rows // channels

    held_rows = database.reshape(-1, E).astype(jnp.float32)
    terms = lax.psum(encoder_terms(held_rows, enc_gain, enc_up, enc_down), "section")
    terms = terms.reshape(blocks_held, halves, channels, quarter, E)
    terms = lax.dynamic_index_in_dim(terms, sec_index, 2, keepdims=False)
    terms = lax.psum_scatter(terms, "mp", scatter_dimension=1, tiled=True)
    terms = lax.all_gather(terms, "section", axis=2, tiled=True)
    terms = terms.reshape(blocks_held, half_rows, E)
    own_rows = lax.dynamic_slice_in_dim(database, mp_index * half_rows, half_rows, 1)
    enc_half = (own_rows.astype(jnp.float32) + terms).astype(jnp.bfloat16)

    id_table = neighbour_ids.reshape(db_count, request)
    owners = id_table // blocks_held
    within = id_table % blocks_held
    places = jnp.arange(request)
    same_owner = owners[:, :, None] == owners[:, None, :]
    earlier = places[None, None, :] < places[None, :, None]
    rank_in = jnp.sum((same_owner & earlier).astype(jnp.int32), axis=-1)
    single = jnp.sum(same_owner.astype(jnp.int32), axis=-1) == 1
    singles_before = jnp.sum((single[:, None, :] & earlier).astype(jnp.int32), axis=-1)
    channel = jnp.where(single, singles_before % channels, rank_in)
    same_channel = channel[:, :, None] == channel[:, None, :]
    slot_in = jnp.sum((same_channel & earlier).astype(jnp.int32), axis=-1)

    serve = (owners == db_index) & (channel == sec_index)
    send_local = jnp.sum(jnp.where(serve, within, 0), axis=-1)
    payload = enc_half[send_local]
    received = lax.all_to_all(payload, "db", split_axis=0, concat_axis=0, tiled=True)

    my_owner = lax.dynamic_index_in_dim(owners, db_index, 0, keepdims=False)
    my_channel = lax.dynamic_index_in_dim(channel, db_index, 0, keepdims=False)
    my_slot = lax.dynamic_index_in_dim(slot_in, db_index, 0, keepdims=False)
    pick = (my_channel[None, :] == sec_index) & (
        my_slot[None, :] == jnp.arange(per_channel)[:, None]
    )
    slot_owner = jnp.sum(jnp.where(pick, my_owner[None, :], 0), axis=-1)
    compact = received[slot_owner]
    channel_blocks = lax.all_gather(compact, "mp", axis=1, tiled=True)
    all_blocks = lax.all_gather(channel_blocks, "section", axis=0, tiled=True)
    flat_pos = my_channel * per_channel + my_slot
    mine = lax.dynamic_slice_in_dim(flat_pos, sec_index * per_channel, per_channel, 0)
    neighbours = all_blocks[mine]
    enc_blocks = neighbours.reshape(-1, NEIGH * NBLOCK, E)

    micro_tokens = hidden_in.shape[0] // channels
    state = lax.dynamic_slice_in_dim(hidden_in, sec_index * micro_tokens, micro_tokens, 0)
    gains = lax.all_gather(dec_gain, "section", axis=0, tiled=True)
    wq = lax.all_gather(w_query, "section", axis=0, tiled=True)
    wk = lax.all_gather(w_key, "section", axis=0, tiled=True)
    wv = lax.all_gather(w_value, "section", axis=0, tiled=True)
    wo = lax.all_gather(w_out, "section", axis=0, tiled=True)
    for layer_id in range(wq.shape[0]):
        state = cross_layer(
            state, enc_blocks, gains[layer_id], wq[layer_id], wk[layer_id], wv[layer_id], wo[layer_id]
        )
    return state


def solution(mesh):
    in_specs = (
        P("db", "mp"),
        P("db", None, None),
        P(),
        P(),
        P(None, ("section", "mp")),
        P(("section", "mp"), None),
        P("section", None),
        P("section", None, "mp"),
        P("section", None, "mp"),
        P("section", None, "mp"),
        P("section", "mp", None),
    )
    out_specs = P(("db", "section"), "mp")
    return jax.shard_map(body, mesh=mesh, in_specs=in_specs, out_specs=out_specs, check_vma=False)
```

```python
import jax
import jax.numpy as jnp
from jax import lax
from jax.sharding import PartitionSpec as P

HD = 128
E = 896
NEIGH = 2
QBLOCK = 64
NBLOCK = 128


def rms_scale(rows_in, gain_vec):
    return (
        rows_in * lax.rsqrt(jnp.mean(rows_in * rows_in, axis=-1, keepdims=True) + 1e-06) * gain_vec
    )


def encoder_terms(floats, enc_gain, enc_up, enc_down):
    normed = rms_scale(floats, enc_gain).astype(jnp.bfloat16)
    inner_act = jax.nn.gelu(
        jnp.dot(normed, enc_up, preferred_element_type=jnp.float32), approximate=True
    ).astype(jnp.bfloat16)
    return jnp.dot(inner_act, enc_down, preferred_element_type=jnp.float32)


def swap(block, axis):
    return lax.ppermute(block, axis, [(0, 1), (1, 0)])


def pair_gather(block, axis, dim):
    other = swap(block, axis)
    first = lax.axis_index(axis) == 0
    return jnp.where(
        first,
        jnp.concatenate([block, other], axis=dim),
        jnp.concatenate([other, block], axis=dim),
    )


def pair_scatter_sum(block, axis, dim, link_type):
    index = lax.axis_index(axis)
    half = block.shape[dim] // 2
    mine = lax.dynamic_slice_in_dim(block, index * half, half, dim)
    theirs = lax.dynamic_slice_in_dim(block, (1 - index) * half, half, dim)
    return mine + swap(theirs.astype(link_type), axis).astype(mine.dtype)


def cross_layer(state_rows, blocks, gain_vec, query_w, key_w, value_w, out_w):
    block_count = blocks.shape[0]
    whole_rows = pair_gather(state_rows, "mp", 1)
    floats = whole_rows.astype(jnp.float32)
    normed = rms_scale(floats, gain_vec).astype(jnp.bfloat16)
    queries = (jnp.dot(normed, query_w, preferred_element_type=jnp.float32) * HD ** (-0.5)).astype(
        jnp.bfloat16
    )
    flat_rows = blocks.reshape(-1, E)
    key_rows = jnp.dot(flat_rows, key_w, preferred_element_type=jnp.float32).astype(jnp.bfloat16)
    value_rows = jnp.dot(flat_rows, value_w, preferred_element_type=jnp.float32).astype(
        jnp.bfloat16
    )
    head_count = query_w.shape[1] // HD
    query_four = queries.reshape(block_count, QBLOCK, head_count, HD)
    key_four = key_rows.reshape(block_count, NEIGH * NBLOCK, head_count, HD)
    value_four = value_rows.reshape(block_count, NEIGH * NBLOCK, head_count, HD)
    scores = jnp.einsum("cqhd,ckhd->chqk", query_four, key_four, preferred_element_type=jnp.float32)
    soft_weights = jax.nn.softmax(scores, axis=-1).astype(jnp.bfloat16)
    context = jnp.einsum(
        "chqk,ckhd->cqhd", soft_weights, value_four, preferred_element_type=jnp.float32
    )
    context = context.astype(jnp.bfloat16).reshape(block_count * QBLOCK, head_count * HD)
    partial_out = jnp.dot(context, out_w, preferred_element_type=jnp.float32)
    head_share = pair_scatter_sum(partial_out, "mp", 1, jnp.bfloat16)
    return (state_rows.astype(jnp.float32) + head_share).astype(jnp.bfloat16)


def body(
    hidden_in,
    database,
    neighbour_ids,
    enc_gain,
    enc_up,
    enc_down,
    dec_gain,
    w_query,
    w_key,
    w_value,
    w_out,
):
    db_count = lax.axis_size("db")
    db_index = lax.axis_index("db")
    channels = lax.axis_size("section")
    sec_index = lax.axis_index("section")
    halves = lax.axis_size("mp")
    mp_index = lax.axis_index("mp")
    blocks_held = database.shape[0]
    request = neighbour_ids.shape[0] // db_count * NEIGH
    per_channel = request // channels
    half_rows = NBLOCK // halves
    quarter = half_rows // channels

    held_rows = database.reshape(-1, E).astype(jnp.float32)
    terms = encoder_terms(held_rows, enc_gain, enc_up, enc_down)
    terms = terms + swap(terms, "section")
    terms = terms.reshape(blocks_held, halves, channels, quarter, E)
    terms = lax.dynamic_index_in_dim(terms, sec_index, 2, keepdims=False)
    terms = pair_scatter_sum(terms, "mp", 1, jnp.float32)
    terms = pair_gather(terms, "section", 2)
    terms = terms.reshape(blocks_held, half_rows, E)
    own_rows = lax.dynamic_slice_in_dim(database, mp_index * half_rows, half_rows, 1)
    enc_half = (own_rows.astype(jnp.float32) + terms).astype(jnp.bfloat16)

    id_table = neighbour_ids.reshape(db_count, request)
    owners = id_table // blocks_held
    within = id_table % blocks_held
    places = jnp.arange(request)
    same_owner = owners[:, :, None] == owners[:, None, :]
    earlier = places[None, None, :] < places[None, :, None]
    rank_in = jnp.sum((same_owner & earlier).astype(jnp.int32), axis=-1)
    single = jnp.sum(same_owner.astype(jnp.int32), axis=-1) == 1
    singles_before = jnp.sum((single[:, None, :] & earlier).astype(jnp.int32), axis=-1)
    channel = jnp.where(single, singles_before % channels, rank_in)
    same_channel = channel[:, :, None] == channel[:, None, :]
    slot_in = jnp.sum((same_channel & earlier).astype(jnp.int32), axis=-1)

    serve = (owners == db_index) & (channel == sec_index)
    send_local = jnp.sum(jnp.where(serve, within, 0), axis=-1)
    payload = enc_half[send_local]
    received = lax.all_to_all(payload, "db", split_axis=0, concat_axis=0, tiled=True)

    my_owner = lax.dynamic_index_in_dim(owners, db_index, 0, keepdims=False)
    my_channel = lax.dynamic_index_in_dim(channel, db_index, 0, keepdims=False)
    my_slot = lax.dynamic_index_in_dim(slot_in, db_index, 0, keepdims=False)
    pick = (my_channel[None, :] == sec_index) & (
        my_slot[None, :] == jnp.arange(per_channel)[:, None]
    )
    slot_owner = jnp.sum(jnp.where(pick, my_owner[None, :], 0), axis=-1)
    compact = received[slot_owner]
    channel_blocks = pair_gather(compact, "mp", 1)
    all_blocks = pair_gather(channel_blocks, "section", 0)
    flat_pos = my_channel * per_channel + my_slot
    mine = lax.dynamic_slice_in_dim(flat_pos, sec_index * per_channel, per_channel, 0)
    neighbours = all_blocks[mine]
    enc_blocks = neighbours.reshape(-1, NEIGH * NBLOCK, E)

    micro_tokens = hidden_in.shape[0] // channels
    state = lax.dynamic_slice_in_dim(hidden_in, sec_index * micro_tokens, micro_tokens, 0)
    gains = lax.all_gather(dec_gain, "section", axis=0, tiled=True)
    wq = lax.all_gather(w_query, "section", axis=0, tiled=True)
    wk = lax.all_gather(w_key, "section", axis=0, tiled=True)
    wv = lax.all_gather(w_value, "section", axis=0, tiled=True)
    wo = lax.all_gather(w_out, "section", axis=0, tiled=True)
    for layer_id in range(wq.shape[0]):
        state = cross_layer(
            state, enc_blocks, gains[layer_id], wq[layer_id], wk[layer_id], wv[layer_id], wo[layer_id]
        )
    return state


def solution(mesh):
    in_specs = (
        P("db", "mp"),
        P("db", None, None),
        P(),
        P(),
        P(None, ("section", "mp")),
        P(("section", "mp"), None),
        P("section", None),
        P("section", None, "mp"),
        P("section", None, "mp"),
        P("section", None, "mp"),
        P("section", "mp", None),
    )
    out_specs = P(("db", "section"), "mp")
    return jax.shard_map(body, mesh=mesh, in_specs=in_specs, out_specs=out_specs, check_vma=False)
```

```python
import jax
import jax.numpy as jnp
from jax import lax
from jax.sharding import PartitionSpec as P

HD = 128
E = 896
NEIGH = 2
QBLOCK = 64
NBLOCK = 128


def rms_scale(rows_in, gain_vec):
    return (
        rows_in * lax.rsqrt(jnp.mean(rows_in * rows_in, axis=-1, keepdims=True) + 1e-06) * gain_vec
    )


def encoder_terms(floats, enc_gain, enc_up, enc_down):
    normed = rms_scale(floats, enc_gain).astype(jnp.bfloat16)
    inner_act = jax.nn.gelu(
        jnp.dot(normed, enc_up, preferred_element_type=jnp.float32), approximate=True
    ).astype(jnp.bfloat16)
    return jnp.dot(inner_act, enc_down, preferred_element_type=jnp.float32)


def swap(block, axis):
    return lax.ppermute(block, axis, [(0, 1), (1, 0)])


def pair_gather(block, axis, dim):
    other = swap(block, axis)
    first = lax.axis_index(axis) == 0
    return jnp.where(
        first,
        jnp.concatenate([block, other], axis=dim),
        jnp.concatenate([other, block], axis=dim),
    )


def pair_scatter_sum(block, axis, dim, link_type):
    index = lax.axis_index(axis)
    half = block.shape[dim] // 2
    mine = lax.dynamic_slice_in_dim(block, index * half, half, dim)
    theirs = lax.dynamic_slice_in_dim(block, (1 - index) * half, half, dim)
    return mine + swap(theirs.astype(link_type), axis).astype(mine.dtype)


def layer_queries(state_rows, gain_vec, query_w):
    whole_rows = pair_gather(state_rows, "mp", 1)
    floats = whole_rows.astype(jnp.float32)
    normed = rms_scale(floats, gain_vec).astype(jnp.bfloat16)
    return (jnp.dot(normed, query_w, preferred_element_type=jnp.float32) * HD ** (-0.5)).astype(
        jnp.bfloat16
    )


def cross_layer(state_rows, queries, blocks, query_w, key_w, value_w, out_w):
    block_count = blocks.shape[0]
    flat_rows = blocks.reshape(-1, E)
    key_rows = jnp.dot(flat_rows, key_w, preferred_element_type=jnp.float32).astype(jnp.bfloat16)
    value_rows = jnp.dot(flat_rows, value_w, preferred_element_type=jnp.float32).astype(
        jnp.bfloat16
    )
    head_count = query_w.shape[1] // HD
    query_four = queries.reshape(block_count, QBLOCK, head_count, HD)
    key_four = key_rows.reshape(block_count, NEIGH * NBLOCK, head_count, HD)
    value_four = value_rows.reshape(block_count, NEIGH * NBLOCK, head_count, HD)
    scores = jnp.einsum("cqhd,ckhd->chqk", query_four, key_four, preferred_element_type=jnp.float32)
    soft_weights = jax.nn.softmax(scores, axis=-1).astype(jnp.bfloat16)
    context = jnp.einsum(
        "chqk,ckhd->cqhd", soft_weights, value_four, preferred_element_type=jnp.float32
    )
    context = context.astype(jnp.bfloat16).reshape(block_count * QBLOCK, head_count * HD)
    partial_out = jnp.dot(context, out_w, preferred_element_type=jnp.float32)
    head_share = pair_scatter_sum(partial_out, "mp", 1, jnp.bfloat16)
    return (state_rows.astype(jnp.float32) + head_share).astype(jnp.bfloat16)


def body(
    hidden_in,
    database,
    neighbour_ids,
    enc_gain,
    enc_up,
    enc_down,
    dec_gain,
    w_query,
    w_key,
    w_value,
    w_out,
):
    db_count = lax.axis_size("db")
    db_index = lax.axis_index("db")
    channels = lax.axis_size("section")
    sec_index = lax.axis_index("section")
    halves = lax.axis_size("mp")
    mp_index = lax.axis_index("mp")
    blocks_held = database.shape[0]
    request = neighbour_ids.shape[0] // db_count * NEIGH
    per_channel = request // channels
    half_rows = NBLOCK // halves
    quarter = half_rows // channels

    wq = lax.all_gather(w_query, "section", axis=0, tiled=True)
    gains = lax.all_gather(dec_gain, "section", axis=0, tiled=True)
    wk = lax.all_gather(w_key, "section", axis=0, tiled=True)
    wv = lax.all_gather(w_value, "section", axis=0, tiled=True)
    wo = lax.all_gather(w_out, "section", axis=0, tiled=True)
    micro_tokens = hidden_in.shape[0] // channels
    state = lax.dynamic_slice_in_dim(hidden_in, sec_index * micro_tokens, micro_tokens, 0)
    queries = layer_queries(state, gains[0], wq[0])

    held_rows = database.reshape(-1, E).astype(jnp.float32)
    terms = encoder_terms(held_rows, enc_gain, enc_up, enc_down)
    terms = terms + swap(terms, "section")
    terms = terms.reshape(blocks_held, halves, channels, quarter, E)
    terms = lax.dynamic_index_in_dim(terms, sec_index, 2, keepdims=False)
    terms = pair_scatter_sum(terms, "mp", 1, jnp.float32)
    terms = pair_gather(terms, "section", 2)
    terms = terms.reshape(blocks_held, half_rows, E)
    own_rows = lax.dynamic_slice_in_dim(database, mp_index * half_rows, half_rows, 1)
    enc_half = (own_rows.astype(jnp.float32) + terms).astype(jnp.bfloat16)

    id_table = neighbour_ids.reshape(db_count, request)
    owners = id_table // blocks_held
    within = id_table % blocks_held
    places = jnp.arange(request)
    same_owner = owners[:, :, None] == owners[:, None, :]
    earlier = places[None, None, :] < places[None, :, None]
    rank_in = jnp.sum((same_owner & earlier).astype(jnp.int32), axis=-1)
    single = jnp.sum(same_owner.astype(jnp.int32), axis=-1) == 1
    singles_before = jnp.sum((single[:, None, :] & earlier).astype(jnp.int32), axis=-1)
    channel = jnp.where(single, singles_before % channels, rank_in)
    same_channel = channel[:, :, None] == channel[:, None, :]
    slot_in = jnp.sum((same_channel & earlier).astype(jnp.int32), axis=-1)

    serve = (owners == db_index) & (channel == sec_index)
    send_local = jnp.sum(jnp.where(serve, within, 0), axis=-1)
    payload = enc_half[send_local]
    received = lax.all_to_all(payload, "db", split_axis=0, concat_axis=0, tiled=True)
    received, queries = lax.optimization_barrier((received, queries))

    my_owner = lax.dynamic_index_in_dim(owners, db_index, 0, keepdims=False)
    my_channel = lax.dynamic_index_in_dim(channel, db_index, 0, keepdims=False)
    my_slot = lax.dynamic_index_in_dim(slot_in, db_index, 0, keepdims=False)
    pick = (my_channel[None, :] == sec_index) & (
        my_slot[None, :] == jnp.arange(per_channel)[:, None]
    )
    slot_owner = jnp.sum(jnp.where(pick, my_owner[None, :], 0), axis=-1)
    compact = received[slot_owner]
    channel_blocks = pair_gather(compact, "mp", 1)
    all_blocks = pair_gather(channel_blocks, "section", 0)
    flat_pos = my_channel * per_channel + my_slot
    mine = lax.dynamic_slice_in_dim(flat_pos, sec_index * per_channel, per_channel, 0)
    neighbours = all_blocks[mine]
    enc_blocks = neighbours.reshape(-1, NEIGH * NBLOCK, E)

    for layer_id in range(wq.shape[0]):
        if layer_id > 0:
            queries = layer_queries(state, gains[layer_id], wq[layer_id])
        state = cross_layer(
            state, queries, enc_blocks, wq[layer_id], wk[layer_id], wv[layer_id], wo[layer_id]
        )
    return state


def solution(mesh):
    in_specs = (
        P("db", "mp"),
        P("db", None, None),
        P(),
        P(),
        P(None, ("section", "mp")),
        P(("section", "mp"), None),
        P("section", None),
        P("section", None, "mp"),
        P("section", None, "mp"),
        P("section", None, "mp"),
        P("section", "mp", None),
    )
    out_specs = P(("db", "section"), "mp")
    return jax.shard_map(body, mesh=mesh, in_specs=in_specs, out_specs=out_specs, check_vma=False)
```

```python
import jax
import jax.numpy as jnp
from jax import lax
from jax.sharding import PartitionSpec as P

HD = 128
E = 896
NEIGH = 2
QBLOCK = 64
NBLOCK = 128


def rms_scale(rows_in, gain_vec):
    return (
        rows_in * lax.rsqrt(jnp.mean(rows_in * rows_in, axis=-1, keepdims=True) + 1e-06) * gain_vec
    )


def encoder_terms(floats, enc_gain, enc_up, enc_down):
    normed = rms_scale(floats, enc_gain).astype(jnp.bfloat16)
    inner_act = jax.nn.gelu(
        jnp.dot(normed, enc_up, preferred_element_type=jnp.float32), approximate=True
    ).astype(jnp.bfloat16)
    return jnp.dot(inner_act, enc_down, preferred_element_type=jnp.float32)


def swap(block, axis):
    return lax.ppermute(block, axis, [(0, 1), (1, 0)])


def pair_gather(block, axis, dim):
    other = swap(block, axis)
    first = lax.axis_index(axis) == 0
    return jnp.where(
        first,
        jnp.concatenate([block, other], axis=dim),
        jnp.concatenate([other, block], axis=dim),
    )


def pair_scatter_sum(block, axis, dim, link_type):
    index = lax.axis_index(axis)
    half = block.shape[dim] // 2
    mine = lax.dynamic_slice_in_dim(block, index * half, half, dim)
    theirs = lax.dynamic_slice_in_dim(block, (1 - index) * half, half, dim)
    return mine + swap(theirs.astype(link_type), axis).astype(mine.dtype)


def layer_queries(state_rows, gain_vec, query_w, whole_rows=None):
    if whole_rows is None:
        whole_rows = pair_gather(state_rows, "mp", 1)
    floats = whole_rows.astype(jnp.float32)
    normed = rms_scale(floats, gain_vec).astype(jnp.bfloat16)
    return (jnp.dot(normed, query_w, preferred_element_type=jnp.float32) * HD ** (-0.5)).astype(
        jnp.bfloat16
    )


def cross_layer(state_rows, queries, blocks, query_w, key_w, value_w, out_w):
    block_count = blocks.shape[0]
    flat_rows = blocks.reshape(-1, E)
    key_rows = jnp.dot(flat_rows, key_w, preferred_element_type=jnp.float32).astype(jnp.bfloat16)
    value_rows = jnp.dot(flat_rows, value_w, preferred_element_type=jnp.float32).astype(
        jnp.bfloat16
    )
    head_count = query_w.shape[1] // HD
    query_four = queries.reshape(block_count, QBLOCK, head_count, HD)
    key_four = key_rows.reshape(block_count, NEIGH * NBLOCK, head_count, HD)
    value_four = value_rows.reshape(block_count, NEIGH * NBLOCK, head_count, HD)
    scores = jnp.einsum("cqhd,ckhd->chqk", query_four, key_four, preferred_element_type=jnp.float32)
    soft_weights = jax.nn.softmax(scores, axis=-1).astype(jnp.bfloat16)
    context = jnp.einsum(
        "chqk,ckhd->cqhd", soft_weights, value_four, preferred_element_type=jnp.float32
    )
    context = context.astype(jnp.bfloat16).reshape(block_count * QBLOCK, head_count * HD)
    partial_out = jnp.dot(context, out_w, preferred_element_type=jnp.float32)
    head_share = pair_scatter_sum(partial_out, "mp", 1, jnp.bfloat16)
    return (state_rows.astype(jnp.float32) + head_share).astype(jnp.bfloat16)


def body(
    hidden_in,
    database,
    neighbour_ids,
    enc_gain,
    enc_up,
    enc_down,
    dec_gain,
    w_query,
    w_key,
    w_value,
    w_out,
):
    db_count = lax.axis_size("db")
    db_index = lax.axis_index("db")
    channels = lax.axis_size("section")
    sec_index = lax.axis_index("section")
    halves = lax.axis_size("mp")
    mp_index = lax.axis_index("mp")
    blocks_held = database.shape[0]
    request = neighbour_ids.shape[0] // db_count * NEIGH
    per_channel = request // channels
    half_rows = NBLOCK // halves
    quarter = half_rows // channels

    wq = lax.all_gather(w_query, "section", axis=0, tiled=True)
    gains = lax.all_gather(dec_gain, "section", axis=0, tiled=True)
    wk = lax.all_gather(w_key, "section", axis=0, tiled=True)
    wv = lax.all_gather(w_value, "section", axis=0, tiled=True)
    wo = lax.all_gather(w_out, "section", axis=0, tiled=True)
    micro_tokens = hidden_in.shape[0] // channels
    state = lax.dynamic_slice_in_dim(hidden_in, sec_index * micro_tokens, micro_tokens, 0)
    first_rows = pair_gather(state, "mp", 1)

    held_rows = database.reshape(-1, E).astype(jnp.float32)
    terms = encoder_terms(held_rows, enc_gain, enc_up, enc_down)
    terms = terms + swap(terms, "section")
    terms = terms.reshape(blocks_held, halves, channels, quarter, E)
    terms = lax.dynamic_index_in_dim(terms, sec_index, 2, keepdims=False)
    terms = pair_scatter_sum(terms, "mp", 1, jnp.float32)
    terms = pair_gather(terms, "section", 2)
    terms = terms.reshape(blocks_held, half_rows, E)
    own_rows = lax.dynamic_slice_in_dim(database, mp_index * half_rows, half_rows, 1)
    enc_half = (own_rows.astype(jnp.float32) + terms).astype(jnp.bfloat16)

    id_table = neighbour_ids.reshape(db_count, request)
    owners = id_table // blocks_held
    within = id_table % blocks_held
    places = jnp.arange(request)
    same_owner = owners[:, :, None] == owners[:, None, :]
    earlier = places[None, None, :] < places[None, :, None]
    rank_in = jnp.sum((same_owner & earlier).astype(jnp.int32), axis=-1)
    single = jnp.sum(same_owner.astype(jnp.int32), axis=-1) == 1
    singles_before = jnp.sum((single[:, None, :] & earlier).astype(jnp.int32), axis=-1)
    channel = jnp.where(single, singles_before % channels, rank_in)
    same_channel = channel[:, :, None] == channel[:, None, :]
    slot_in = jnp.sum((same_channel & earlier).astype(jnp.int32), axis=-1)

    serve = (owners == db_index) & (channel == sec_index)
    send_local = jnp.sum(jnp.where(serve, within, 0), axis=-1)
    payload = enc_half[send_local]
    payload, first_rows = lax.optimization_barrier((payload, first_rows))
    queries = layer_queries(state, gains[0], wq[0], first_rows)
    received = lax.all_to_all(payload, "db", split_axis=0, concat_axis=0, tiled=True)
    received, queries = lax.optimization_barrier((received, queries))

    my_owner = lax.dynamic_index_in_dim(owners, db_index, 0, keepdims=False)
    my_channel = lax.dynamic_index_in_dim(channel, db_index, 0, keepdims=False)
    my_slot = lax.dynamic_index_in_dim(slot_in, db_index, 0, keepdims=False)
    pick = (my_channel[None, :] == sec_index) & (
        my_slot[None, :] == jnp.arange(per_channel)[:, None]
    )
    slot_owner = jnp.sum(jnp.where(pick, my_owner[None, :], 0), axis=-1)
    compact = received[slot_owner]
    channel_blocks = pair_gather(compact, "mp", 1)
    all_blocks = pair_gather(channel_blocks, "section", 0)
    flat_pos = my_channel * per_channel + my_slot
    mine = lax.dynamic_slice_in_dim(flat_pos, sec_index * per_channel, per_channel, 0)
    neighbours = all_blocks[mine]
    enc_blocks = neighbours.reshape(-1, NEIGH * NBLOCK, E)

    for layer_id in range(wq.shape[0]):
        if layer_id > 0:
            queries = layer_queries(state, gains[layer_id], wq[layer_id])
        state = cross_layer(
            state, queries, enc_blocks, wq[layer_id], wk[layer_id], wv[layer_id], wo[layer_id]
        )
    return state


def solution(mesh):
    in_specs = (
        P("db", "mp"),
        P("db", None, None),
        P(),
        P(),
        P(None, ("section", "mp")),
        P(("section", "mp"), None),
        P("section", None),
        P("section", None, "mp"),
        P("section", None, "mp"),
        P("section", None, "mp"),
        P("section", "mp", None),
    )
    out_specs = P(("db", "section"), "mp")
    return jax.shard_map(body, mesh=mesh, in_specs=in_specs, out_specs=out_specs, check_vma=False)
```

```python
import jax
import jax.numpy as jnp
from jax import lax
from jax.sharding import PartitionSpec as P

HD = 128
E = 896
NEIGH = 2
QBLOCK = 64
NBLOCK = 128


def rms_scale(rows_in, gain_vec):
    return (
        rows_in * lax.rsqrt(jnp.mean(rows_in * rows_in, axis=-1, keepdims=True) + 1e-06) * gain_vec
    )


def encoder_terms(floats, enc_gain, enc_up, enc_down):
    normed = rms_scale(floats, enc_gain).astype(jnp.bfloat16)
    inner_act = jax.nn.gelu(
        jnp.dot(normed, enc_up, preferred_element_type=jnp.float32), approximate=True
    ).astype(jnp.bfloat16)
    return jnp.dot(inner_act, enc_down, preferred_element_type=jnp.float32)


def swap(block, axis):
    return lax.ppermute(block, axis, [(0, 1), (1, 0)])


def pair_gather(block, axis, dim):
    other = swap(block, axis)
    first = lax.axis_index(axis) == 0
    return jnp.where(
        first,
        jnp.concatenate([block, other], axis=dim),
        jnp.concatenate([other, block], axis=dim),
    )


def pair_scatter_sum(block, axis, dim, link_type):
    index = lax.axis_index(axis)
    half = block.shape[dim] // 2
    mine = lax.dynamic_slice_in_dim(block, index * half, half, dim)
    theirs = lax.dynamic_slice_in_dim(block, (1 - index) * half, half, dim)
    return mine + swap(theirs.astype(link_type), axis).astype(mine.dtype)


def layer_queries(state_rows, gain_vec, query_w, whole_rows=None):
    if whole_rows is None:
        whole_rows = pair_gather(state_rows, "mp", 1)
    floats = whole_rows.astype(jnp.float32)
    normed = rms_scale(floats, gain_vec).astype(jnp.bfloat16)
    return (jnp.dot(normed, query_w, preferred_element_type=jnp.float32) * HD ** (-0.5)).astype(
        jnp.bfloat16
    )


def cross_layer(state_rows, queries, blocks, query_w, key_w, value_w, out_w):
    block_count = blocks.shape[0]
    flat_rows = blocks.reshape(-1, E)
    key_rows = jnp.dot(flat_rows, key_w, preferred_element_type=jnp.float32).astype(jnp.bfloat16)
    value_rows = jnp.dot(flat_rows, value_w, preferred_element_type=jnp.float32).astype(
        jnp.bfloat16
    )
    head_count = query_w.shape[1] // HD
    query_four = queries.reshape(block_count, QBLOCK, head_count, HD)
    key_four = key_rows.reshape(block_count, NEIGH * NBLOCK, head_count, HD)
    value_four = value_rows.reshape(block_count, NEIGH * NBLOCK, head_count, HD)
    scores = jnp.einsum("cqhd,ckhd->chqk", query_four, key_four, preferred_element_type=jnp.float32)
    soft_weights = jax.nn.softmax(scores, axis=-1).astype(jnp.bfloat16)
    context = jnp.einsum(
        "chqk,ckhd->cqhd", soft_weights, value_four, preferred_element_type=jnp.float32
    )
    context = context.astype(jnp.bfloat16).reshape(block_count * QBLOCK, head_count * HD)
    partial_out = jnp.dot(context, out_w, preferred_element_type=jnp.float32)
    head_share = pair_scatter_sum(partial_out, "mp", 1, jnp.bfloat16)
    return (state_rows.astype(jnp.float32) + head_share).astype(jnp.bfloat16)


def body(
    hidden_in,
    database,
    neighbour_ids,
    enc_gain,
    enc_up,
    enc_down,
    dec_gain,
    w_query,
    w_key,
    w_value,
    w_out,
):
    db_count = lax.axis_size("db")
    db_index = lax.axis_index("db")
    channels = lax.axis_size("section")
    sec_index = lax.axis_index("section")
    halves = lax.axis_size("mp")
    mp_index = lax.axis_index("mp")
    blocks_held = database.shape[0]
    request = neighbour_ids.shape[0] // db_count * NEIGH
    per_channel = request // channels
    half_rows = NBLOCK // halves
    quarter = half_rows // channels

    wq = lax.all_gather(w_query, "section", axis=0, tiled=True)
    gains = lax.all_gather(dec_gain, "section", axis=0, tiled=True)
    wk = lax.all_gather(w_key, "section", axis=0, tiled=True)
    wv = lax.all_gather(w_value, "section", axis=0, tiled=True)
    wo = lax.all_gather(w_out, "section", axis=0, tiled=True)
    micro_tokens = hidden_in.shape[0] // channels
    state = lax.dynamic_slice_in_dim(hidden_in, sec_index * micro_tokens, micro_tokens, 0)
    first_rows = pair_gather(state, "mp", 1)

    held_rows = database.reshape(-1, E).astype(jnp.float32)
    terms = encoder_terms(held_rows, enc_gain, enc_up, enc_down)
    terms = terms + swap(terms, "section")
    terms = terms.reshape(blocks_held, halves, channels, quarter, E)
    terms = lax.dynamic_index_in_dim(terms, sec_index, 2, keepdims=False)
    terms = pair_scatter_sum(terms, "mp", 1, jnp.float32)
    terms = pair_gather(terms, "section", 2)
    terms = terms.reshape(blocks_held, half_rows, E)
    own_rows = lax.dynamic_slice_in_dim(database, mp_index * half_rows, half_rows, 1)
    enc_half = (own_rows.astype(jnp.float32) + terms).astype(jnp.bfloat16)

    id_table = neighbour_ids.reshape(db_count, request)
    owners = id_table // blocks_held
    within = id_table % blocks_held
    places = jnp.arange(request)
    same_owner = owners[:, :, None] == owners[:, None, :]
    earlier = places[None, None, :] < places[None, :, None]
    rank_in = jnp.sum((same_owner & earlier).astype(jnp.int32), axis=-1)
    single = jnp.sum(same_owner.astype(jnp.int32), axis=-1) == 1
    singles_before = jnp.sum((single[:, None, :] & earlier).astype(jnp.int32), axis=-1)
    channel = jnp.where(single, singles_before % channels, rank_in)
    same_channel = channel[:, :, None] == channel[:, None, :]
    slot_in = jnp.sum((same_channel & earlier).astype(jnp.int32), axis=-1)

    serve = (owners == db_index) & (channel == sec_index)
    send_local = jnp.sum(jnp.where(serve, within, 0), axis=-1)
    payload = enc_half[send_local]
    payload, first_rows = lax.optimization_barrier((payload, first_rows))
    queries = layer_queries(state, gains[0], wq[0], first_rows)
    received = lax.all_to_all(payload, "db", split_axis=0, concat_axis=0, tiled=True)
    received, queries = lax.optimization_barrier((received, queries))

    my_owner = lax.dynamic_index_in_dim(owners, db_index, 0, keepdims=False)
    my_channel = lax.dynamic_index_in_dim(channel, db_index, 0, keepdims=False)
    my_slot = lax.dynamic_index_in_dim(slot_in, db_index, 0, keepdims=False)
    pick = (my_channel[None, :] == sec_index) & (
        my_slot[None, :] == jnp.arange(per_channel)[:, None]
    )
    slot_owner = jnp.sum(jnp.where(pick, my_owner[None, :], 0), axis=-1)
    compact = received[slot_owner]
    channel_blocks = pair_gather(compact, "mp", 1)
    all_blocks = pair_gather(channel_blocks, "section", 0)
    flat_pos = my_channel * per_channel + my_slot
    mine = lax.dynamic_slice_in_dim(flat_pos, sec_index * per_channel, per_channel, 0)
    neighbours = all_blocks[mine]
    enc_blocks = neighbours.reshape(-1, NEIGH * NBLOCK, E)

    batches = 2
    batch_tokens = micro_tokens // batches
    batch_blocks = enc_blocks.shape[0] // batches
    states = [state[i * batch_tokens : (i + 1) * batch_tokens] for i in range(batches)]
    batch_queries = [queries[i * batch_tokens : (i + 1) * batch_tokens] for i in range(batches)]
    batch_neighbours = [
        enc_blocks[i * batch_blocks : (i + 1) * batch_blocks] for i in range(batches)
    ]
    for layer_id in range(wq.shape[0]):
        for i in range(batches):
            if layer_id > 0:
                batch_queries[i] = layer_queries(states[i], gains[layer_id], wq[layer_id])
            states[i] = cross_layer(
                states[i],
                batch_queries[i],
                batch_neighbours[i],
                wq[layer_id],
                wk[layer_id],
                wv[layer_id],
                wo[layer_id],
            )
    return jnp.concatenate(states, axis=0)


def solution(mesh):
    in_specs = (
        P("db", "mp"),
        P("db", None, None),
        P(),
        P(),
        P(None, ("section", "mp")),
        P(("section", "mp"), None),
        P("section", None),
        P("section", None, "mp"),
        P("section", None, "mp"),
        P("section", None, "mp"),
        P("section", "mp", None),
    )
    out_specs = P(("db", "section"), "mp")
    return jax.shard_map(body, mesh=mesh, in_specs=in_specs, out_specs=out_specs, check_vma=False)
```

```python
import jax
import jax.numpy as jnp
from jax import lax
from jax.sharding import PartitionSpec as P

HD = 128
E = 896
NEIGH = 2
QBLOCK = 64
NBLOCK = 128


def rms_scale(rows_in, gain_vec):
    return (
        rows_in * lax.rsqrt(jnp.mean(rows_in * rows_in, axis=-1, keepdims=True) + 1e-06) * gain_vec
    )


def encoder_terms(floats, enc_gain, enc_up, enc_down):
    normed = rms_scale(floats, enc_gain).astype(jnp.bfloat16)
    inner_act = jax.nn.gelu(
        jnp.dot(normed, enc_up, preferred_element_type=jnp.float32), approximate=True
    ).astype(jnp.bfloat16)
    return jnp.dot(inner_act, enc_down, preferred_element_type=jnp.float32)


def swap(block, axis):
    return lax.ppermute(block, axis, [(0, 1), (1, 0)])


def pair_gather(block, axis, dim):
    other = swap(block, axis)
    first = lax.axis_index(axis) == 0
    return jnp.where(
        first,
        jnp.concatenate([block, other], axis=dim),
        jnp.concatenate([other, block], axis=dim),
    )


def pair_scatter_sum(block, axis, dim, link_type):
    index = lax.axis_index(axis)
    half = block.shape[dim] // 2
    mine = lax.dynamic_slice_in_dim(block, index * half, half, dim)
    theirs = lax.dynamic_slice_in_dim(block, (1 - index) * half, half, dim)
    return mine + swap(theirs.astype(link_type), axis).astype(mine.dtype)


def layer_queries(state_rows, gain_vec, query_w, whole_rows=None):
    if whole_rows is None:
        whole_rows = pair_gather(state_rows, "mp", 1)
    floats = whole_rows.astype(jnp.float32)
    normed = rms_scale(floats, gain_vec).astype(jnp.bfloat16)
    return (jnp.dot(normed, query_w, preferred_element_type=jnp.float32) * HD ** (-0.5)).astype(
        jnp.bfloat16
    )


def cross_layer(state_rows, queries, blocks, query_w, key_w, value_w, out_w):
    block_count = blocks.shape[0]
    flat_rows = blocks.reshape(-1, E)
    key_rows = jnp.dot(flat_rows, key_w, preferred_element_type=jnp.float32).astype(jnp.bfloat16)
    value_rows = jnp.dot(flat_rows, value_w, preferred_element_type=jnp.float32).astype(
        jnp.bfloat16
    )
    head_count = query_w.shape[1] // HD
    query_four = queries.reshape(block_count, QBLOCK, head_count, HD)
    key_four = key_rows.reshape(block_count, NEIGH * NBLOCK, head_count, HD)
    value_four = value_rows.reshape(block_count, NEIGH * NBLOCK, head_count, HD)
    scores = jnp.einsum("cqhd,ckhd->chqk", query_four, key_four, preferred_element_type=jnp.float32)
    soft_weights = jax.nn.softmax(scores, axis=-1).astype(jnp.bfloat16)
    context = jnp.einsum(
        "chqk,ckhd->cqhd", soft_weights, value_four, preferred_element_type=jnp.float32
    )
    context = context.astype(jnp.bfloat16).reshape(block_count * QBLOCK, head_count * HD)
    partial_out = jnp.dot(context, out_w, preferred_element_type=jnp.float32)
    head_share = pair_scatter_sum(partial_out, "mp", 1, jnp.bfloat16)
    return (state_rows.astype(jnp.float32) + head_share).astype(jnp.bfloat16)


def body(
    hidden_in,
    database,
    neighbour_ids,
    enc_gain,
    enc_up,
    enc_down,
    dec_gain,
    w_query,
    w_key,
    w_value,
    w_out,
):
    db_count = lax.axis_size("db")
    db_index = lax.axis_index("db")
    channels = lax.axis_size("section")
    sec_index = lax.axis_index("section")
    halves = lax.axis_size("mp")
    mp_index = lax.axis_index("mp")
    blocks_held = database.shape[0]
    request = neighbour_ids.shape[0] // db_count * NEIGH
    per_channel = request // channels
    half_rows = NBLOCK // halves
    quarter = half_rows // channels

    wq = lax.optimization_barrier(pair_gather(w_query, "section", 0))
    gains = pair_gather(dec_gain, "section", 0)
    wk = lax.optimization_barrier(pair_gather(w_key, "section", 0))
    wv = lax.optimization_barrier(pair_gather(w_value, "section", 0))
    wo = lax.optimization_barrier(pair_gather(w_out, "section", 0))
    micro_tokens = hidden_in.shape[0] // channels
    state = lax.dynamic_slice_in_dim(hidden_in, sec_index * micro_tokens, micro_tokens, 0)
    first_rows = pair_gather(state, "mp", 1)

    held_rows = database.reshape(-1, E).astype(jnp.float32)
    terms = encoder_terms(held_rows, enc_gain, enc_up, enc_down)
    terms = terms + swap(terms, "section")
    terms = terms.reshape(blocks_held, halves, channels, quarter, E)
    terms = lax.dynamic_index_in_dim(terms, sec_index, 2, keepdims=False)
    terms = pair_scatter_sum(terms, "mp", 1, jnp.float32)
    terms = pair_gather(terms, "section", 2)
    terms = terms.reshape(blocks_held, half_rows, E)
    own_rows = lax.dynamic_slice_in_dim(database, mp_index * half_rows, half_rows, 1)
    enc_half = (own_rows.astype(jnp.float32) + terms).astype(jnp.bfloat16)

    id_table = neighbour_ids.reshape(db_count, request)
    owners = id_table // blocks_held
    within = id_table % blocks_held
    places = jnp.arange(request)
    same_owner = owners[:, :, None] == owners[:, None, :]
    earlier = places[None, None, :] < places[None, :, None]
    rank_in = jnp.sum((same_owner & earlier).astype(jnp.int32), axis=-1)
    single = jnp.sum(same_owner.astype(jnp.int32), axis=-1) == 1
    singles_before = jnp.sum((single[:, None, :] & earlier).astype(jnp.int32), axis=-1)
    channel = jnp.where(single, singles_before % channels, rank_in)
    same_channel = channel[:, :, None] == channel[:, None, :]
    slot_in = jnp.sum((same_channel & earlier).astype(jnp.int32), axis=-1)

    serve = (owners == db_index) & (channel == sec_index)
    send_local = jnp.sum(jnp.where(serve, within, 0), axis=-1)
    payload = enc_half[send_local]
    payload, first_rows = lax.optimization_barrier((payload, first_rows))
    queries = layer_queries(state, gains[0], wq[0], first_rows)
    received = lax.all_to_all(payload, "db", split_axis=0, concat_axis=0, tiled=True)
    received, queries = lax.optimization_barrier((received, queries))

    my_owner = lax.dynamic_index_in_dim(owners, db_index, 0, keepdims=False)
    my_channel = lax.dynamic_index_in_dim(channel, db_index, 0, keepdims=False)
    my_slot = lax.dynamic_index_in_dim(slot_in, db_index, 0, keepdims=False)
    pick = (my_channel[None, :] == sec_index) & (
        my_slot[None, :] == jnp.arange(per_channel)[:, None]
    )
    slot_owner = jnp.sum(jnp.where(pick, my_owner[None, :], 0), axis=-1)
    compact = received[slot_owner]
    channel_blocks = pair_gather(compact, "mp", 1)
    all_blocks = pair_gather(channel_blocks, "section", 0)
    flat_pos = my_channel * per_channel + my_slot
    mine = lax.dynamic_slice_in_dim(flat_pos, sec_index * per_channel, per_channel, 0)
    neighbours = all_blocks[mine]
    enc_blocks = neighbours.reshape(-1, NEIGH * NBLOCK, E)

    batches = 2
    batch_tokens = micro_tokens // batches
    batch_blocks = enc_blocks.shape[0] // batches
    states = [state[i * batch_tokens : (i + 1) * batch_tokens] for i in range(batches)]
    batch_queries = [queries[i * batch_tokens : (i + 1) * batch_tokens] for i in range(batches)]
    batch_neighbours = [
        enc_blocks[i * batch_blocks : (i + 1) * batch_blocks] for i in range(batches)
    ]
    for layer_id in range(wq.shape[0]):
        for i in range(batches):
            if layer_id > 0:
                batch_queries[i] = layer_queries(states[i], gains[layer_id], wq[layer_id])
            states[i] = cross_layer(
                states[i],
                batch_queries[i],
                batch_neighbours[i],
                wq[layer_id],
                wk[layer_id],
                wv[layer_id],
                wo[layer_id],
            )
    return jnp.concatenate(states, axis=0)


def solution(mesh):
    in_specs = (
        P("db", "mp"),
        P("db", None, None),
        P(),
        P(),
        P(None, ("section", "mp")),
        P(("section", "mp"), None),
        P("section", None),
        P("section", None, "mp"),
        P("section", None, "mp"),
        P("section", None, "mp"),
        P("section", "mp", None),
    )
    out_specs = P(("db", "section"), "mp")
    return jax.shard_map(body, mesh=mesh, in_specs=in_specs, out_specs=out_specs, check_vma=False)
```

```python
import jax
import jax.numpy as jnp
from jax import lax
from jax.sharding import PartitionSpec as P

HD = 128
E = 896
NEIGH = 2
QBLOCK = 64
NBLOCK = 128


def rms_scale(rows_in, gain_vec):
    return (
        rows_in * lax.rsqrt(jnp.mean(rows_in * rows_in, axis=-1, keepdims=True) + 1e-06) * gain_vec
    )


def encoder_terms(floats, enc_gain, enc_up, enc_down):
    normed = rms_scale(floats, enc_gain).astype(jnp.bfloat16)
    inner_act = jax.nn.gelu(
        jnp.dot(normed, enc_up, preferred_element_type=jnp.float32), approximate=True
    ).astype(jnp.bfloat16)
    return jnp.dot(inner_act, enc_down, preferred_element_type=jnp.float32)


def swap(block, axis):
    return lax.ppermute(block, axis, [(0, 1), (1, 0)])


def pair_gather(block, axis, dim):
    other = swap(block, axis)
    first = lax.axis_index(axis) == 0
    return jnp.where(
        first,
        jnp.concatenate([block, other], axis=dim),
        jnp.concatenate([other, block], axis=dim),
    )


def pair_scatter_sum(block, axis, dim, link_type):
    index = lax.axis_index(axis)
    half = block.shape[dim] // 2
    mine = lax.dynamic_slice_in_dim(block, index * half, half, dim)
    theirs = lax.dynamic_slice_in_dim(block, (1 - index) * half, half, dim)
    return mine + swap(theirs.astype(link_type), axis).astype(mine.dtype)


def layer_queries(state_rows, gain_vec, query_w, whole_rows=None):
    if whole_rows is None:
        whole_rows = pair_gather(state_rows, "mp", 1)
    floats = whole_rows.astype(jnp.float32)
    normed = rms_scale(floats, gain_vec).astype(jnp.bfloat16)
    return (jnp.dot(normed, query_w, preferred_element_type=jnp.float32) * HD ** (-0.5)).astype(
        jnp.bfloat16
    )


def cross_layer(state_rows, queries, blocks, query_w, key_w, value_w, out_w):
    block_count = blocks.shape[0]
    flat_rows = blocks.reshape(-1, E)
    key_rows = jnp.dot(flat_rows, key_w, preferred_element_type=jnp.float32).astype(jnp.bfloat16)
    value_rows = jnp.dot(flat_rows, value_w, preferred_element_type=jnp.float32).astype(
        jnp.bfloat16
    )
    head_count = query_w.shape[1] // HD
    query_four = queries.reshape(block_count, QBLOCK, head_count, HD)
    key_four = key_rows.reshape(block_count, NEIGH * NBLOCK, head_count, HD)
    value_four = value_rows.reshape(block_count, NEIGH * NBLOCK, head_count, HD)
    scores = jnp.einsum("cqhd,ckhd->chqk", query_four, key_four, preferred_element_type=jnp.float32)
    soft_weights = jax.nn.softmax(scores, axis=-1).astype(jnp.bfloat16)
    context = jnp.einsum(
        "chqk,ckhd->cqhd", soft_weights, value_four, preferred_element_type=jnp.float32
    )
    context = context.astype(jnp.bfloat16).reshape(block_count * QBLOCK, head_count * HD)
    partial_out = jnp.dot(context, out_w, preferred_element_type=jnp.float32)
    head_share = pair_scatter_sum(partial_out, "mp", 1, jnp.bfloat16)
    return (state_rows.astype(jnp.float32) + head_share).astype(jnp.bfloat16)


def body(
    hidden_in,
    database,
    neighbour_ids,
    enc_gain,
    enc_up,
    enc_down,
    dec_gain,
    w_query,
    w_key,
    w_value,
    w_out,
):
    db_count = lax.axis_size("db")
    db_index = lax.axis_index("db")
    channels = lax.axis_size("section")
    sec_index = lax.axis_index("section")
    halves = lax.axis_size("mp")
    mp_index = lax.axis_index("mp")
    blocks_held = database.shape[0]
    request = neighbour_ids.shape[0] // db_count * NEIGH
    per_channel = request // channels
    half_rows = NBLOCK // halves
    quarter = half_rows // channels

    wq = lax.optimization_barrier(pair_gather(w_query, "section", 0))
    gains = pair_gather(dec_gain, "section", 0)
    wk = lax.optimization_barrier(pair_gather(w_key, "section", 0))
    wv = lax.optimization_barrier(pair_gather(w_value, "section", 0))
    wo = lax.optimization_barrier(pair_gather(w_out, "section", 0))
    micro_tokens = hidden_in.shape[0] // channels
    state = lax.dynamic_slice_in_dim(hidden_in, sec_index * micro_tokens, micro_tokens, 0)
    first_rows = pair_gather(state, "mp", 1)

    held_rows = database.reshape(-1, E).astype(jnp.float32)
    terms = encoder_terms(held_rows, enc_gain, enc_up, enc_down)
    terms = terms + swap(terms, "section")
    terms = terms.reshape(blocks_held, halves, channels, quarter, E)
    terms = lax.dynamic_index_in_dim(terms, sec_index, 2, keepdims=False)
    terms = pair_scatter_sum(terms, "mp", 1, jnp.float32)
    terms = pair_gather(terms, "section", 2)
    terms = terms.reshape(blocks_held, half_rows, E)
    own_rows = lax.dynamic_slice_in_dim(database, mp_index * half_rows, half_rows, 1)
    enc_half = (own_rows.astype(jnp.float32) + terms).astype(jnp.bfloat16)

    id_table = neighbour_ids.reshape(db_count, request)
    owners = id_table // blocks_held
    within = id_table % blocks_held
    places = jnp.arange(request)
    same_owner = owners[:, :, None] == owners[:, None, :]
    earlier = places[None, None, :] < places[None, :, None]
    rank_in = jnp.sum((same_owner & earlier).astype(jnp.int32), axis=-1)
    single = jnp.sum(same_owner.astype(jnp.int32), axis=-1) == 1
    singles_before = jnp.sum((single[:, None, :] & earlier).astype(jnp.int32), axis=-1)
    channel = jnp.where(single, singles_before % channels, rank_in)
    same_channel = channel[:, :, None] == channel[:, None, :]
    slot_in = jnp.sum((same_channel & earlier).astype(jnp.int32), axis=-1)

    serve = (owners == db_index) & (channel == sec_index)
    send_local = jnp.sum(jnp.where(serve, within, 0), axis=-1)
    payload = enc_half[send_local]
    payload, first_rows = lax.optimization_barrier((payload, first_rows))
    queries = layer_queries(state, gains[0], wq[0], first_rows)
    received = lax.all_to_all(payload, "db", split_axis=0, concat_axis=0, tiled=True)
    received, queries, wk, wv, wo = lax.optimization_barrier((received, queries, wk, wv, wo))

    my_owner = lax.dynamic_index_in_dim(owners, db_index, 0, keepdims=False)
    my_channel = lax.dynamic_index_in_dim(channel, db_index, 0, keepdims=False)
    my_slot = lax.dynamic_index_in_dim(slot_in, db_index, 0, keepdims=False)
    pick = (my_channel[None, :] == sec_index) & (
        my_slot[None, :] == jnp.arange(per_channel)[:, None]
    )
    slot_owner = jnp.sum(jnp.where(pick, my_owner[None, :], 0), axis=-1)
    compact = received[slot_owner]
    channel_blocks = pair_gather(compact, "mp", 1)
    all_blocks = pair_gather(channel_blocks, "section", 0)
    flat_pos = my_channel * per_channel + my_slot
    mine = lax.dynamic_slice_in_dim(flat_pos, sec_index * per_channel, per_channel, 0)
    neighbours = all_blocks[mine]
    enc_blocks = neighbours.reshape(-1, NEIGH * NBLOCK, E)

    batches = 2
    batch_tokens = micro_tokens // batches
    batch_blocks = enc_blocks.shape[0] // batches
    states = [state[i * batch_tokens : (i + 1) * batch_tokens] for i in range(batches)]
    batch_queries = [queries[i * batch_tokens : (i + 1) * batch_tokens] for i in range(batches)]
    batch_neighbours = [
        enc_blocks[i * batch_blocks : (i + 1) * batch_blocks] for i in range(batches)
    ]
    for layer_id in range(wq.shape[0]):
        for i in range(batches):
            if layer_id > 0:
                batch_queries[i] = layer_queries(states[i], gains[layer_id], wq[layer_id])
            states[i] = cross_layer(
                states[i],
                batch_queries[i],
                batch_neighbours[i],
                wq[layer_id],
                wk[layer_id],
                wv[layer_id],
                wo[layer_id],
            )
    return jnp.concatenate(states, axis=0)


def solution(mesh):
    in_specs = (
        P("db", "mp"),
        P("db", None, None),
        P(),
        P(),
        P(None, ("section", "mp")),
        P(("section", "mp"), None),
        P("section", None),
        P("section", None, "mp"),
        P("section", None, "mp"),
        P("section", None, "mp"),
        P("section", "mp", None),
    )
    out_specs = P(("db", "section"), "mp")
    return jax.shard_map(body, mesh=mesh, in_specs=in_specs, out_specs=out_specs, check_vma=False)
```

```python
import jax
import jax.numpy as jnp
from jax import lax
from jax.sharding import PartitionSpec as P

HD = 128
E = 896
NEIGH = 2
QBLOCK = 64
NBLOCK = 128


def rms_scale(rows_in, gain_vec):
    return (
        rows_in * lax.rsqrt(jnp.mean(rows_in * rows_in, axis=-1, keepdims=True) + 1e-06) * gain_vec
    )


def encoder_terms(floats, enc_gain, enc_up, enc_down):
    normed = rms_scale(floats, enc_gain).astype(jnp.bfloat16)
    inner_act = jax.nn.gelu(
        jnp.dot(normed, enc_up, preferred_element_type=jnp.float32), approximate=True
    ).astype(jnp.bfloat16)
    return jnp.dot(inner_act, enc_down, preferred_element_type=jnp.float32)


def swap(block, axis):
    return lax.ppermute(block, axis, [(0, 1), (1, 0)])


def pair_gather(block, axis, dim):
    other = swap(block, axis)
    first = lax.axis_index(axis) == 0
    return jnp.where(
        first,
        jnp.concatenate([block, other], axis=dim),
        jnp.concatenate([other, block], axis=dim),
    )


def pair_scatter_sum(block, axis, dim, link_type):
    index = lax.axis_index(axis)
    half = block.shape[dim] // 2
    mine = lax.dynamic_slice_in_dim(block, index * half, half, dim)
    theirs = lax.dynamic_slice_in_dim(block, (1 - index) * half, half, dim)
    return mine + swap(theirs.astype(link_type), axis).astype(mine.dtype)


def layer_queries(state_rows, gain_vec, query_w, whole_rows=None):
    if whole_rows is None:
        whole_rows = pair_gather(state_rows, "mp", 1)
    floats = whole_rows.astype(jnp.float32)
    normed = rms_scale(floats, gain_vec).astype(jnp.bfloat16)
    return (jnp.dot(normed, query_w, preferred_element_type=jnp.float32) * HD ** (-0.5)).astype(
        jnp.bfloat16
    )


def cross_layer(state_rows, queries, blocks, query_w, key_w, value_w, out_w):
    block_count = blocks.shape[0]
    flat_rows = blocks.reshape(-1, E)
    key_rows = jnp.dot(flat_rows, key_w, preferred_element_type=jnp.float32).astype(jnp.bfloat16)
    value_rows = jnp.dot(flat_rows, value_w, preferred_element_type=jnp.float32).astype(
        jnp.bfloat16
    )
    head_count = query_w.shape[1] // HD
    query_four = queries.reshape(block_count, QBLOCK, head_count, HD)
    key_four = key_rows.reshape(block_count, NEIGH * NBLOCK, head_count, HD)
    value_four = value_rows.reshape(block_count, NEIGH * NBLOCK, head_count, HD)
    scores = jnp.einsum("cqhd,ckhd->chqk", query_four, key_four, preferred_element_type=jnp.float32)
    soft_weights = jax.nn.softmax(scores, axis=-1).astype(jnp.bfloat16)
    context = jnp.einsum(
        "chqk,ckhd->cqhd", soft_weights, value_four, preferred_element_type=jnp.float32
    )
    context = context.astype(jnp.bfloat16).reshape(block_count * QBLOCK, head_count * HD)
    partial_out = jnp.dot(context, out_w, preferred_element_type=jnp.float32)
    head_share = pair_scatter_sum(partial_out, "mp", 1, jnp.bfloat16)
    return (state_rows.astype(jnp.float32) + head_share).astype(jnp.bfloat16)


def body(
    hidden_in,
    database,
    neighbour_ids,
    enc_gain,
    enc_up,
    enc_down,
    dec_gain,
    w_query,
    w_key,
    w_value,
    w_out,
):
    db_count = lax.axis_size("db")
    db_index = lax.axis_index("db")
    channels = lax.axis_size("section")
    sec_index = lax.axis_index("section")
    halves = lax.axis_size("mp")
    mp_index = lax.axis_index("mp")
    blocks_held = database.shape[0]
    request = neighbour_ids.shape[0] // db_count * NEIGH
    per_channel = request // channels
    half_rows = NBLOCK // halves
    quarter = half_rows // channels

    gains = pair_gather(dec_gain, "section", 0)
    micro_tokens = hidden_in.shape[0] // channels
    state = lax.dynamic_slice_in_dim(hidden_in, sec_index * micro_tokens, micro_tokens, 0)
    first_rows = pair_gather(state, "mp", 1)

    held_rows = database.reshape(-1, E).astype(jnp.float32)
    terms = encoder_terms(held_rows, enc_gain, enc_up, enc_down)
    terms = terms + swap(terms, "section")
    terms = terms.reshape(blocks_held, halves, channels, quarter, E)
    terms = lax.dynamic_index_in_dim(terms, sec_index, 2, keepdims=False)
    terms, first_rows = lax.optimization_barrier((terms, first_rows))
    terms = pair_scatter_sum(terms, "mp", 1, jnp.float32)
    terms = pair_gather(terms, "section", 2)

    terms, w_query, w_key, w_value, w_out = lax.optimization_barrier(
        (terms, w_query, w_key, w_value, w_out)
    )
    wq = lax.optimization_barrier(pair_gather(w_query, "section", 0))
    wk = lax.optimization_barrier(pair_gather(w_key, "section", 0))
    wv = lax.optimization_barrier(pair_gather(w_value, "section", 0))
    wo = lax.optimization_barrier(pair_gather(w_out, "section", 0))
    terms = terms.reshape(blocks_held, half_rows, E)
    own_rows = lax.dynamic_slice_in_dim(database, mp_index * half_rows, half_rows, 1)
    enc_half = (own_rows.astype(jnp.float32) + terms).astype(jnp.bfloat16)

    id_table = neighbour_ids.reshape(db_count, request)
    owners = id_table // blocks_held
    within = id_table % blocks_held
    places = jnp.arange(request)
    same_owner = owners[:, :, None] == owners[:, None, :]
    earlier = places[None, None, :] < places[None, :, None]
    rank_in = jnp.sum((same_owner & earlier).astype(jnp.int32), axis=-1)
    single = jnp.sum(same_owner.astype(jnp.int32), axis=-1) == 1
    singles_before = jnp.sum((single[:, None, :] & earlier).astype(jnp.int32), axis=-1)
    channel = jnp.where(single, singles_before % channels, rank_in)
    same_channel = channel[:, :, None] == channel[:, None, :]
    slot_in = jnp.sum((same_channel & earlier).astype(jnp.int32), axis=-1)

    serve = (owners == db_index) & (channel == sec_index)
    send_local = jnp.sum(jnp.where(serve, within, 0), axis=-1)
    payload = enc_half[send_local]
    payload, first_rows = lax.optimization_barrier((payload, first_rows))
    queries = layer_queries(state, gains[0], wq[0], first_rows)
    received = lax.all_to_all(payload, "db", split_axis=0, concat_axis=0, tiled=True)
    received, queries, wk, wv, wo = lax.optimization_barrier((received, queries, wk, wv, wo))

    my_owner = lax.dynamic_index_in_dim(owners, db_index, 0, keepdims=False)
    my_channel = lax.dynamic_index_in_dim(channel, db_index, 0, keepdims=False)
    my_slot = lax.dynamic_index_in_dim(slot_in, db_index, 0, keepdims=False)
    pick = (my_channel[None, :] == sec_index) & (
        my_slot[None, :] == jnp.arange(per_channel)[:, None]
    )
    slot_owner = jnp.sum(jnp.where(pick, my_owner[None, :], 0), axis=-1)
    compact = received[slot_owner]
    channel_blocks = pair_gather(compact, "mp", 1)
    all_blocks = pair_gather(channel_blocks, "section", 0)
    flat_pos = my_channel * per_channel + my_slot
    mine = lax.dynamic_slice_in_dim(flat_pos, sec_index * per_channel, per_channel, 0)
    neighbours = all_blocks[mine]
    enc_blocks = neighbours.reshape(-1, NEIGH * NBLOCK, E)

    batches = 2
    batch_tokens = micro_tokens // batches
    batch_blocks = enc_blocks.shape[0] // batches
    states = [state[i * batch_tokens : (i + 1) * batch_tokens] for i in range(batches)]
    batch_queries = [queries[i * batch_tokens : (i + 1) * batch_tokens] for i in range(batches)]
    batch_neighbours = [
        enc_blocks[i * batch_blocks : (i + 1) * batch_blocks] for i in range(batches)
    ]
    for layer_id in range(wq.shape[0]):
        for i in range(batches):
            if layer_id > 0:
                batch_queries[i] = layer_queries(states[i], gains[layer_id], wq[layer_id])
            states[i] = cross_layer(
                states[i],
                batch_queries[i],
                batch_neighbours[i],
                wq[layer_id],
                wk[layer_id],
                wv[layer_id],
                wo[layer_id],
            )
    return jnp.concatenate(states, axis=0)


def solution(mesh):
    in_specs = (
        P("db", "mp"),
        P("db", None, None),
        P(),
        P(),
        P(None, ("section", "mp")),
        P(("section", "mp"), None),
        P("section", None),
        P("section", None, "mp"),
        P("section", None, "mp"),
        P("section", None, "mp"),
        P("section", "mp", None),
    )
    out_specs = P(("db", "section"), "mp")
    return jax.shard_map(body, mesh=mesh, in_specs=in_specs, out_specs=out_specs, check_vma=False)
```

```python
import jax
import jax.numpy as jnp
from jax import lax
from jax.sharding import PartitionSpec as P

HD = 128
E = 896
NEIGH = 2
QBLOCK = 64
NBLOCK = 128


def rms_scale(rows_in, gain_vec):
    return (
        rows_in * lax.rsqrt(jnp.mean(rows_in * rows_in, axis=-1, keepdims=True) + 1e-06) * gain_vec
    )


def encoder_terms(floats, enc_gain, enc_up, enc_down):
    normed = rms_scale(floats, enc_gain).astype(jnp.bfloat16)
    inner_act = jax.nn.gelu(
        jnp.dot(normed, enc_up, preferred_element_type=jnp.float32), approximate=True
    ).astype(jnp.bfloat16)
    return jnp.dot(inner_act, enc_down, preferred_element_type=jnp.float32)


def swap(block, axis):
    return lax.ppermute(block, axis, [(0, 1), (1, 0)])


def pair_gather(block, axis, dim):
    other = swap(block, axis)
    first = lax.axis_index(axis) == 0
    return jnp.where(
        first,
        jnp.concatenate([block, other], axis=dim),
        jnp.concatenate([other, block], axis=dim),
    )


def pair_scatter_sum(block, axis, dim, link_type):
    index = lax.axis_index(axis)
    half = block.shape[dim] // 2
    mine = lax.dynamic_slice_in_dim(block, index * half, half, dim)
    theirs = lax.dynamic_slice_in_dim(block, (1 - index) * half, half, dim)
    return mine + swap(theirs.astype(link_type), axis).astype(mine.dtype)


def layer_queries(state_rows, gain_vec, query_w, whole_rows=None):
    if whole_rows is None:
        whole_rows = pair_gather(state_rows, "mp", 1)
    floats = whole_rows.astype(jnp.float32)
    normed = rms_scale(floats, gain_vec).astype(jnp.bfloat16)
    return (jnp.dot(normed, query_w, preferred_element_type=jnp.float32) * HD ** (-0.5)).astype(
        jnp.bfloat16
    )


def cross_layer(state_rows, queries, blocks, query_w, key_w, value_w, out_w):
    block_count = blocks.shape[0]
    flat_rows = blocks.reshape(-1, E)
    key_rows = jnp.dot(flat_rows, key_w, preferred_element_type=jnp.float32).astype(jnp.bfloat16)
    value_rows = jnp.dot(flat_rows, value_w, preferred_element_type=jnp.float32).astype(
        jnp.bfloat16
    )
    head_count = query_w.shape[1] // HD
    query_four = queries.reshape(block_count, QBLOCK, head_count, HD)
    key_four = key_rows.reshape(block_count, NEIGH * NBLOCK, head_count, HD)
    value_four = value_rows.reshape(block_count, NEIGH * NBLOCK, head_count, HD)
    scores = jnp.einsum("cqhd,ckhd->chqk", query_four, key_four, preferred_element_type=jnp.float32)
    soft_weights = jax.nn.softmax(scores, axis=-1).astype(jnp.bfloat16)
    context = jnp.einsum(
        "chqk,ckhd->cqhd", soft_weights, value_four, preferred_element_type=jnp.float32
    )
    context = context.astype(jnp.bfloat16).reshape(block_count * QBLOCK, head_count * HD)
    partial_out = jnp.dot(context, out_w, preferred_element_type=jnp.float32)
    head_share = pair_scatter_sum(partial_out, "mp", 1, jnp.bfloat16)
    return (state_rows.astype(jnp.float32) + head_share).astype(jnp.bfloat16)


def body(
    hidden_in,
    database,
    neighbour_ids,
    enc_gain,
    enc_up,
    enc_down,
    dec_gain,
    w_query,
    w_key,
    w_value,
    w_out,
):
    db_count = lax.axis_size("db")
    db_index = lax.axis_index("db")
    channels = lax.axis_size("section")
    sec_index = lax.axis_index("section")
    halves = lax.axis_size("mp")
    mp_index = lax.axis_index("mp")
    blocks_held = database.shape[0]
    request = neighbour_ids.shape[0] // db_count * NEIGH
    per_channel = request // channels
    half_rows = NBLOCK // halves
    quarter = half_rows // channels

    gains = pair_gather(dec_gain, "section", 0)
    gains, w_query, w_key, w_value, w_out = lax.optimization_barrier(
        (gains, w_query, w_key, w_value, w_out)
    )
    wq = lax.optimization_barrier(pair_gather(w_query, "section", 0))
    wk = lax.optimization_barrier(pair_gather(w_key, "section", 0))
    wv = lax.optimization_barrier(pair_gather(w_value, "section", 0))
    wo = lax.optimization_barrier(pair_gather(w_out, "section", 0))
    micro_tokens = hidden_in.shape[0] // channels
    state = lax.dynamic_slice_in_dim(hidden_in, sec_index * micro_tokens, micro_tokens, 0)
    first_rows = pair_gather(state, "mp", 1)

    held_rows = database.reshape(-1, E).astype(jnp.float32)
    terms = encoder_terms(held_rows, enc_gain, enc_up, enc_down)
    terms = terms + swap(terms, "section")
    terms = terms.reshape(blocks_held, halves, channels, quarter, E)
    terms = lax.dynamic_index_in_dim(terms, sec_index, 2, keepdims=False)
    terms = pair_scatter_sum(terms, "mp", 1, jnp.float32)
    terms = pair_gather(terms, "section", 2)
    terms = terms.reshape(blocks_held, half_rows, E)
    own_rows = lax.dynamic_slice_in_dim(database, mp_index * half_rows, half_rows, 1)
    enc_half = (own_rows.astype(jnp.float32) + terms).astype(jnp.bfloat16)

    id_table = neighbour_ids.reshape(db_count, request)
    owners = id_table // blocks_held
    within = id_table % blocks_held
    places = jnp.arange(request)
    same_owner = owners[:, :, None] == owners[:, None, :]
    earlier = places[None, None, :] < places[None, :, None]
    rank_in = jnp.sum((same_owner & earlier).astype(jnp.int32), axis=-1)
    single = jnp.sum(same_owner.astype(jnp.int32), axis=-1) == 1
    singles_before = jnp.sum((single[:, None, :] & earlier).astype(jnp.int32), axis=-1)
    channel = jnp.where(single, singles_before % channels, rank_in)
    same_channel = channel[:, :, None] == channel[:, None, :]
    slot_in = jnp.sum((same_channel & earlier).astype(jnp.int32), axis=-1)

    serve = (owners == db_index) & (channel == sec_index)
    send_local = jnp.sum(jnp.where(serve, within, 0), axis=-1)
    payload = enc_half[send_local]
    payload, first_rows = lax.optimization_barrier((payload, first_rows))
    queries = layer_queries(state, gains[0], wq[0], first_rows)
    received = lax.all_to_all(payload, "db", split_axis=0, concat_axis=0, tiled=True)
    received, queries, wk, wv, wo = lax.optimization_barrier((received, queries, wk, wv, wo))

    my_owner = lax.dynamic_index_in_dim(owners, db_index, 0, keepdims=False)
    my_channel = lax.dynamic_index_in_dim(channel, db_index, 0, keepdims=False)
    my_slot = lax.dynamic_index_in_dim(slot_in, db_index, 0, keepdims=False)
    pick = (my_channel[None, :] == sec_index) & (
        my_slot[None, :] == jnp.arange(per_channel)[:, None]
    )
    slot_owner = jnp.sum(jnp.where(pick, my_owner[None, :], 0), axis=-1)
    compact = received[slot_owner]
    channel_blocks = pair_gather(compact, "mp", 1)
    all_blocks = pair_gather(channel_blocks, "section", 0)
    flat_pos = my_channel * per_channel + my_slot
    mine = lax.dynamic_slice_in_dim(flat_pos, sec_index * per_channel, per_channel, 0)
    neighbours = all_blocks[mine]
    enc_blocks = neighbours.reshape(-1, NEIGH * NBLOCK, E)

    batches = 2
    batch_tokens = micro_tokens // batches
    batch_blocks = enc_blocks.shape[0] // batches
    states = [state[i * batch_tokens : (i + 1) * batch_tokens] for i in range(batches)]
    batch_queries = [queries[i * batch_tokens : (i + 1) * batch_tokens] for i in range(batches)]
    batch_neighbours = [
        enc_blocks[i * batch_blocks : (i + 1) * batch_blocks] for i in range(batches)
    ]
    for layer_id in range(wq.shape[0]):
        for i in range(batches):
            if layer_id > 0:
                batch_queries[i] = layer_queries(states[i], gains[layer_id], wq[layer_id])
            states[i] = cross_layer(
                states[i],
                batch_queries[i],
                batch_neighbours[i],
                wq[layer_id],
                wk[layer_id],
                wv[layer_id],
                wo[layer_id],
            )
    return jnp.concatenate(states, axis=0)


def solution(mesh):
    in_specs = (
        P("db", "mp"),
        P("db", None, None),
        P(),
        P(),
        P(None, ("section", "mp")),
        P(("section", "mp"), None),
        P("section", None),
        P("section", None, "mp"),
        P("section", None, "mp"),
        P("section", None, "mp"),
        P("section", "mp", None),
    )
    out_specs = P(("db", "section"), "mp")
    return jax.shard_map(body, mesh=mesh, in_specs=in_specs, out_specs=out_specs, check_vma=False)
```

```python
import jax
import jax.numpy as jnp
from jax import lax
from jax.sharding import PartitionSpec as P

HD = 128
E = 896
NEIGH = 2
QBLOCK = 64
NBLOCK = 128


def rms_scale(rows_in, gain_vec):
    return (
        rows_in * lax.rsqrt(jnp.mean(rows_in * rows_in, axis=-1, keepdims=True) + 1e-06) * gain_vec
    )


def encoder_terms(floats, enc_gain, enc_up, enc_down):
    normed = rms_scale(floats, enc_gain).astype(jnp.bfloat16)
    inner_act = jax.nn.gelu(
        jnp.dot(normed, enc_up, preferred_element_type=jnp.float32), approximate=True
    ).astype(jnp.bfloat16)
    return jnp.dot(inner_act, enc_down, preferred_element_type=jnp.float32)


def swap(block, axis):
    return lax.ppermute(block, axis, [(0, 1), (1, 0)])


def pair_gather(block, axis, dim):
    other = swap(block, axis)
    first = lax.axis_index(axis) == 0
    return jnp.where(
        first,
        jnp.concatenate([block, other], axis=dim),
        jnp.concatenate([other, block], axis=dim),
    )


def pair_scatter_sum(block, axis, dim, link_type):
    index = lax.axis_index(axis)
    half = block.shape[dim] // 2
    mine = lax.dynamic_slice_in_dim(block, index * half, half, dim)
    theirs = lax.dynamic_slice_in_dim(block, (1 - index) * half, half, dim)
    return mine + swap(theirs.astype(link_type), axis).astype(mine.dtype)


def layer_queries(state_rows, gain_vec, query_w, whole_rows=None):
    if whole_rows is None:
        whole_rows = pair_gather(state_rows, "mp", 1)
    floats = whole_rows.astype(jnp.float32)
    normed = rms_scale(floats, gain_vec).astype(jnp.bfloat16)
    return (jnp.dot(normed, query_w, preferred_element_type=jnp.float32) * HD ** (-0.5)).astype(
        jnp.bfloat16
    )


def cross_layer(state_rows, queries, blocks, query_w, key_w, value_w, out_w):
    block_count = blocks.shape[0]
    flat_rows = blocks.reshape(-1, E)
    key_rows = jnp.dot(flat_rows, key_w, preferred_element_type=jnp.float32).astype(jnp.bfloat16)
    value_rows = jnp.dot(flat_rows, value_w, preferred_element_type=jnp.float32).astype(
        jnp.bfloat16
    )
    head_count = query_w.shape[1] // HD
    query_four = queries.reshape(block_count, QBLOCK, head_count, HD)
    key_four = key_rows.reshape(block_count, NEIGH * NBLOCK, head_count, HD)
    value_four = value_rows.reshape(block_count, NEIGH * NBLOCK, head_count, HD)
    scores = jnp.einsum("cqhd,ckhd->chqk", query_four, key_four, preferred_element_type=jnp.float32)
    soft_weights = jax.nn.softmax(scores, axis=-1).astype(jnp.bfloat16)
    context = jnp.einsum(
        "chqk,ckhd->cqhd", soft_weights, value_four, preferred_element_type=jnp.float32
    )
    context = context.astype(jnp.bfloat16).reshape(block_count * QBLOCK, head_count * HD)
    partial_out = jnp.dot(context, out_w, preferred_element_type=jnp.float32)
    head_share = pair_scatter_sum(partial_out, "mp", 1, jnp.bfloat16)
    return (state_rows.astype(jnp.float32) + head_share).astype(jnp.bfloat16)


def body(
    hidden_in,
    database,
    neighbour_ids,
    enc_gain,
    enc_up,
    enc_down,
    dec_gain,
    w_query,
    w_key,
    w_value,
    w_out,
):
    db_count = lax.axis_size("db")
    db_index = lax.axis_index("db")
    channels = lax.axis_size("section")
    sec_index = lax.axis_index("section")
    halves = lax.axis_size("mp")
    mp_index = lax.axis_index("mp")
    blocks_held = database.shape[0]
    request = neighbour_ids.shape[0] // db_count * NEIGH
    per_channel = request // channels
    half_rows = NBLOCK // halves

    gains = pair_gather(dec_gain, "section", 0)
    micro_tokens = hidden_in.shape[0] // channels
    state = lax.dynamic_slice_in_dim(hidden_in, sec_index * micro_tokens, micro_tokens, 0)
    first_rows = pair_gather(state, "mp", 1)

    held_rows = database.reshape(-1, E).astype(jnp.float32)
    terms = encoder_terms(held_rows, enc_gain, enc_up, enc_down)
    terms = terms + swap(terms, "section")
    terms, gains, w_query, w_key, w_value, w_out = lax.optimization_barrier(
        (terms, gains, w_query, w_key, w_value, w_out)
    )
    wq = lax.optimization_barrier(pair_gather(w_query, "section", 0))
    wk = lax.optimization_barrier(pair_gather(w_key, "section", 0))
    wv = lax.optimization_barrier(pair_gather(w_value, "section", 0))
    wo = lax.optimization_barrier(pair_gather(w_out, "section", 0))
    terms = terms.reshape(blocks_held, halves, half_rows, E)
    terms = pair_scatter_sum(terms, "mp", 1, jnp.bfloat16)
    terms = terms.reshape(blocks_held, half_rows, E)
    own_rows = lax.dynamic_slice_in_dim(database, mp_index * half_rows, half_rows, 1)
    enc_half = (own_rows.astype(jnp.float32) + terms).astype(jnp.bfloat16)

    id_table = neighbour_ids.reshape(db_count, request)
    owners = id_table // blocks_held
    within = id_table % blocks_held
    places = jnp.arange(request)
    same_owner = owners[:, :, None] == owners[:, None, :]
    earlier = places[None, None, :] < places[None, :, None]
    rank_in = jnp.sum((same_owner & earlier).astype(jnp.int32), axis=-1)
    single = jnp.sum(same_owner.astype(jnp.int32), axis=-1) == 1
    singles_before = jnp.sum((single[:, None, :] & earlier).astype(jnp.int32), axis=-1)
    channel = jnp.where(single, singles_before % channels, rank_in)
    same_channel = channel[:, :, None] == channel[:, None, :]
    slot_in = jnp.sum((same_channel & earlier).astype(jnp.int32), axis=-1)

    serve = (owners == db_index) & (channel == sec_index)
    send_local = jnp.sum(jnp.where(serve, within, 0), axis=-1)
    payload = enc_half[send_local]
    payload, first_rows = lax.optimization_barrier((payload, first_rows))
    queries = layer_queries(state, gains[0], wq[0], first_rows)
    received = lax.all_to_all(payload, "db", split_axis=0, concat_axis=0, tiled=True)
    received, queries, wk, wv, wo = lax.optimization_barrier((received, queries, wk, wv, wo))

    my_owner = lax.dynamic_index_in_dim(owners, db_index, 0, keepdims=False)
    my_channel = lax.dynamic_index_in_dim(channel, db_index, 0, keepdims=False)
    my_slot = lax.dynamic_index_in_dim(slot_in, db_index, 0, keepdims=False)
    pick = (my_channel[None, :] == sec_index) & (
        my_slot[None, :] == jnp.arange(per_channel)[:, None]
    )
    slot_owner = jnp.sum(jnp.where(pick, my_owner[None, :], 0), axis=-1)
    compact = received[slot_owner]
    channel_blocks = pair_gather(compact, "mp", 1)
    all_blocks = pair_gather(channel_blocks, "section", 0)
    flat_pos = my_channel * per_channel + my_slot
    mine = lax.dynamic_slice_in_dim(flat_pos, sec_index * per_channel, per_channel, 0)
    neighbours = all_blocks[mine]
    enc_blocks = neighbours.reshape(-1, NEIGH * NBLOCK, E)

    batches = 2
    batch_tokens = micro_tokens // batches
    batch_blocks = enc_blocks.shape[0] // batches
    states = [state[i * batch_tokens : (i + 1) * batch_tokens] for i in range(batches)]
    batch_queries = [queries[i * batch_tokens : (i + 1) * batch_tokens] for i in range(batches)]
    batch_neighbours = [
        enc_blocks[i * batch_blocks : (i + 1) * batch_blocks] for i in range(batches)
    ]
    for layer_id in range(wq.shape[0]):
        for i in range(batches):
            if layer_id > 0:
                batch_queries[i] = layer_queries(states[i], gains[layer_id], wq[layer_id])
            states[i] = cross_layer(
                states[i],
                batch_queries[i],
                batch_neighbours[i],
                wq[layer_id],
                wk[layer_id],
                wv[layer_id],
                wo[layer_id],
            )
    return jnp.concatenate(states, axis=0)


def solution(mesh):
    in_specs = (
        P("db", "mp"),
        P("db", None, None),
        P(),
        P(),
        P(None, ("section", "mp")),
        P(("section", "mp"), None),
        P("section", None),
        P("section", None, "mp"),
        P("section", None, "mp"),
        P("section", None, "mp"),
        P("section", "mp", None),
    )
    out_specs = P(("db", "section"), "mp")
    return jax.shard_map(body, mesh=mesh, in_specs=in_specs, out_specs=out_specs, check_vma=False)
```

```python
import jax
import jax.numpy as jnp
from jax import lax
from jax.sharding import PartitionSpec as P

HD = 128
E = 896
NEIGH = 2
QBLOCK = 64
NBLOCK = 128


def rms_scale(rows_in, gain_vec):
    return (
        rows_in * lax.rsqrt(jnp.mean(rows_in * rows_in, axis=-1, keepdims=True) + 1e-06) * gain_vec
    )


def encoder_terms(floats, enc_gain, enc_up, enc_down):
    normed = rms_scale(floats, enc_gain).astype(jnp.bfloat16)
    inner_act = jax.nn.gelu(
        jnp.dot(normed, enc_up, preferred_element_type=jnp.float32), approximate=True
    ).astype(jnp.bfloat16)
    return jnp.dot(inner_act, enc_down, preferred_element_type=jnp.float32)


def swap(block, axis):
    return lax.ppermute(block, axis, [(0, 1), (1, 0)])


def pair_gather(block, axis, dim):
    other = swap(block, axis)
    first = lax.axis_index(axis) == 0
    return jnp.where(
        first,
        jnp.concatenate([block, other], axis=dim),
        jnp.concatenate([other, block], axis=dim),
    )


def layer_stack(own, axis):
    other = swap(own, axis)
    first = lax.axis_index(axis) == 0
    return lax.cond(first, lambda a, b: (a, b), lambda a, b: (b, a), own, other)


def pair_scatter_sum(block, axis, dim, link_type):
    index = lax.axis_index(axis)
    half = block.shape[dim] // 2
    mine = lax.dynamic_slice_in_dim(block, index * half, half, dim)
    theirs = lax.dynamic_slice_in_dim(block, (1 - index) * half, half, dim)
    return mine + swap(theirs.astype(link_type), axis).astype(mine.dtype)


def layer_queries(state_rows, gain_vec, query_w, whole_rows=None):
    if whole_rows is None:
        whole_rows = pair_gather(state_rows, "mp", 1)
    floats = whole_rows.astype(jnp.float32)
    normed = rms_scale(floats, gain_vec).astype(jnp.bfloat16)
    return (jnp.dot(normed, query_w, preferred_element_type=jnp.float32) * HD ** (-0.5)).astype(
        jnp.bfloat16
    )


def cross_layer(state_rows, queries, blocks, query_w, key_w, value_w, out_w):
    block_count = blocks.shape[0]
    flat_rows = blocks.reshape(-1, E)
    key_rows = jnp.dot(flat_rows, key_w, preferred_element_type=jnp.float32).astype(jnp.bfloat16)
    value_rows = jnp.dot(flat_rows, value_w, preferred_element_type=jnp.float32).astype(
        jnp.bfloat16
    )
    head_count = query_w.shape[1] // HD
    query_four = queries.reshape(block_count, QBLOCK, head_count, HD)
    key_four = key_rows.reshape(block_count, NEIGH * NBLOCK, head_count, HD)
    value_four = value_rows.reshape(block_count, NEIGH * NBLOCK, head_count, HD)
    scores = jnp.einsum("cqhd,ckhd->chqk", query_four, key_four, preferred_element_type=jnp.float32)
    soft_weights = jax.nn.softmax(scores, axis=-1).astype(jnp.bfloat16)
    context = jnp.einsum(
        "chqk,ckhd->cqhd", soft_weights, value_four, preferred_element_type=jnp.float32
    )
    context = context.astype(jnp.bfloat16).reshape(block_count * QBLOCK, head_count * HD)
    partial_out = jnp.dot(context, out_w, preferred_element_type=jnp.float32)
    head_share = pair_scatter_sum(partial_out, "mp", 1, jnp.bfloat16)
    return (state_rows.astype(jnp.float32) + head_share).astype(jnp.bfloat16)


def body(
    hidden_in,
    database,
    neighbour_ids,
    enc_gain,
    enc_up,
    enc_down,
    dec_gain,
    w_query,
    w_key,
    w_value,
    w_out,
):
    db_count = lax.axis_size("db")
    db_index = lax.axis_index("db")
    channels = lax.axis_size("section")
    sec_index = lax.axis_index("section")
    halves = lax.axis_size("mp")
    mp_index = lax.axis_index("mp")
    blocks_held = database.shape[0]
    request = neighbour_ids.shape[0] // db_count * NEIGH
    per_channel = request // channels
    half_rows = NBLOCK // halves

    gains = pair_gather(dec_gain, "section", 0)
    micro_tokens = hidden_in.shape[0] // channels
    state = lax.dynamic_slice_in_dim(hidden_in, sec_index * micro_tokens, micro_tokens, 0)
    first_rows = pair_gather(state, "mp", 1)

    held_rows = database.reshape(-1, E).astype(jnp.float32)
    terms = encoder_terms(held_rows, enc_gain, enc_up, enc_down)
    terms = terms + swap(terms, "section")
    terms, gains, w_query, w_key, w_value, w_out = lax.optimization_barrier(
        (terms, gains, w_query, w_key, w_value, w_out)
    )
    wq = layer_stack(w_query[0], "section")
    wk = layer_stack(w_key[0], "section")
    wv = layer_stack(w_value[0], "section")
    wo = layer_stack(w_out[0], "section")
    terms = terms.reshape(blocks_held, halves, half_rows, E)
    terms = pair_scatter_sum(terms, "mp", 1, jnp.bfloat16)
    terms = terms.reshape(blocks_held, half_rows, E)
    own_rows = lax.dynamic_slice_in_dim(database, mp_index * half_rows, half_rows, 1)
    enc_half = (own_rows.astype(jnp.float32) + terms).astype(jnp.bfloat16)

    id_table = neighbour_ids.reshape(db_count, request)
    owners = id_table // blocks_held
    within = id_table % blocks_held
    places = jnp.arange(request)
    same_owner = owners[:, :, None] == owners[:, None, :]
    earlier = places[None, None, :] < places[None, :, None]
    rank_in = jnp.sum((same_owner & earlier).astype(jnp.int32), axis=-1)
    single = jnp.sum(same_owner.astype(jnp.int32), axis=-1) == 1
    singles_before = jnp.sum((single[:, None, :] & earlier).astype(jnp.int32), axis=-1)
    channel = jnp.where(single, singles_before % channels, rank_in)
    same_channel = channel[:, :, None] == channel[:, None, :]
    slot_in = jnp.sum((same_channel & earlier).astype(jnp.int32), axis=-1)

    serve = (owners == db_index) & (channel == sec_index)
    send_local = jnp.sum(jnp.where(serve, within, 0), axis=-1)
    payload = enc_half[send_local]
    payload, first_rows = lax.optimization_barrier((payload, first_rows))
    queries = layer_queries(state, gains[0], wq[0], first_rows)
    received = lax.all_to_all(payload, "db", split_axis=0, concat_axis=0, tiled=True)
    received, queries, wk, wv, wo = lax.optimization_barrier((received, queries, wk, wv, wo))

    my_owner = lax.dynamic_index_in_dim(owners, db_index, 0, keepdims=False)
    my_channel = lax.dynamic_index_in_dim(channel, db_index, 0, keepdims=False)
    my_slot = lax.dynamic_index_in_dim(slot_in, db_index, 0, keepdims=False)
    pick = (my_channel[None, :] == sec_index) & (
        my_slot[None, :] == jnp.arange(per_channel)[:, None]
    )
    slot_owner = jnp.sum(jnp.where(pick, my_owner[None, :], 0), axis=-1)
    compact = received[slot_owner]
    channel_blocks = pair_gather(compact, "mp", 1)
    all_blocks = pair_gather(channel_blocks, "section", 0)
    flat_pos = my_channel * per_channel + my_slot
    mine = lax.dynamic_slice_in_dim(flat_pos, sec_index * per_channel, per_channel, 0)
    neighbours = all_blocks[mine]
    enc_blocks = neighbours.reshape(-1, NEIGH * NBLOCK, E)

    batches = 2
    batch_tokens = micro_tokens // batches
    batch_blocks = enc_blocks.shape[0] // batches
    states = [state[i * batch_tokens : (i + 1) * batch_tokens] for i in range(batches)]
    batch_queries = [queries[i * batch_tokens : (i + 1) * batch_tokens] for i in range(batches)]
    batch_neighbours = [
        enc_blocks[i * batch_blocks : (i + 1) * batch_blocks] for i in range(batches)
    ]
    for layer_id in range(len(wq)):
        for i in range(batches):
            if layer_id > 0:
                batch_queries[i] = layer_queries(states[i], gains[layer_id], wq[layer_id])
            states[i] = cross_layer(
                states[i],
                batch_queries[i],
                batch_neighbours[i],
                wq[layer_id],
                wk[layer_id],
                wv[layer_id],
                wo[layer_id],
            )
    return jnp.concatenate(states, axis=0)


def solution(mesh):
    in_specs = (
        P("db", "mp"),
        P("db", None, None),
        P(),
        P(),
        P(None, ("section", "mp")),
        P(("section", "mp"), None),
        P("section", None),
        P("section", None, "mp"),
        P("section", None, "mp"),
        P("section", None, "mp"),
        P("section", "mp", None),
    )
    out_specs = P(("db", "section"), "mp")
    return jax.shard_map(body, mesh=mesh, in_specs=in_specs, out_specs=out_specs, check_vma=False)
```

```python
import jax
import jax.numpy as jnp
from jax import lax
from jax.sharding import PartitionSpec as P

HD = 128
E = 896
NEIGH = 2
QBLOCK = 64
NBLOCK = 128


def rms_scale(rows_in, gain_vec):
    return (
        rows_in * lax.rsqrt(jnp.mean(rows_in * rows_in, axis=-1, keepdims=True) + 1e-06) * gain_vec
    )


def encoder_terms(floats, enc_gain, enc_up, enc_down):
    normed = rms_scale(floats, enc_gain).astype(jnp.bfloat16)
    inner_act = jax.nn.gelu(
        jnp.dot(normed, enc_up, preferred_element_type=jnp.float32), approximate=True
    ).astype(jnp.bfloat16)
    return jnp.dot(inner_act, enc_down, preferred_element_type=jnp.float32)


def swap(block, axis):
    return lax.ppermute(block, axis, [(0, 1), (1, 0)])


def pair_gather(block, axis, dim):
    other = swap(block, axis)
    first = lax.axis_index(axis) == 0
    return jnp.where(
        first,
        jnp.concatenate([block, other], axis=dim),
        jnp.concatenate([other, block], axis=dim),
    )


def pair_scatter_sum(block, axis, dim, link_type):
    index = lax.axis_index(axis)
    half = block.shape[dim] // 2
    mine = lax.dynamic_slice_in_dim(block, index * half, half, dim)
    theirs = lax.dynamic_slice_in_dim(block, (1 - index) * half, half, dim)
    return mine + swap(theirs.astype(link_type), axis).astype(mine.dtype)


def layer_queries(state_rows, gain_vec, query_w, whole_rows=None):
    if whole_rows is None:
        whole_rows = pair_gather(state_rows, "mp", 1)
    floats = whole_rows.astype(jnp.float32)
    normed = rms_scale(floats, gain_vec).astype(jnp.bfloat16)
    return (jnp.dot(normed, query_w, preferred_element_type=jnp.float32) * HD ** (-0.5)).astype(
        jnp.bfloat16
    )


def cross_layer(state_rows, queries, blocks, query_w, key_w, value_w, out_w):
    block_count = blocks.shape[0]
    flat_rows = blocks.reshape(-1, E)
    key_rows = jnp.dot(flat_rows, key_w, preferred_element_type=jnp.float32).astype(jnp.bfloat16)
    value_rows = jnp.dot(flat_rows, value_w, preferred_element_type=jnp.float32).astype(
        jnp.bfloat16
    )
    head_count = query_w.shape[1] // HD
    query_four = queries.reshape(block_count, QBLOCK, head_count, HD)
    key_four = key_rows.reshape(block_count, NEIGH * NBLOCK, head_count, HD)
    value_four = value_rows.reshape(block_count, NEIGH * NBLOCK, head_count, HD)
    scores = jnp.einsum("cqhd,ckhd->chqk", query_four, key_four, preferred_element_type=jnp.float32)
    soft_weights = jax.nn.softmax(scores, axis=-1).astype(jnp.bfloat16)
    context = jnp.einsum(
        "chqk,ckhd->cqhd", soft_weights, value_four, preferred_element_type=jnp.float32
    )
    context = context.astype(jnp.bfloat16).reshape(block_count * QBLOCK, head_count * HD)
    partial_out = jnp.dot(context, out_w, preferred_element_type=jnp.float32)
    head_share = pair_scatter_sum(partial_out, "mp", 1, jnp.bfloat16)
    return (state_rows.astype(jnp.float32) + head_share).astype(jnp.bfloat16)


def body(
    hidden_in,
    database,
    neighbour_ids,
    enc_gain,
    enc_up,
    enc_down,
    dec_gain,
    w_query,
    w_key,
    w_value,
    w_out,
):
    db_count = lax.axis_size("db")
    db_index = lax.axis_index("db")
    channels = lax.axis_size("section")
    sec_index = lax.axis_index("section")
    halves = lax.axis_size("mp")
    mp_index = lax.axis_index("mp")
    blocks_held = database.shape[0]
    request = neighbour_ids.shape[0] // db_count * NEIGH
    per_channel = request // channels
    half_rows = NBLOCK // halves

    gains = pair_gather(dec_gain, "section", 0)
    micro_tokens = hidden_in.shape[0] // channels
    state = lax.dynamic_slice_in_dim(hidden_in, sec_index * micro_tokens, micro_tokens, 0)
    first_rows = pair_gather(state, "mp", 1)

    held_rows = database.reshape(-1, E).astype(jnp.float32)
    terms = encoder_terms(held_rows, enc_gain, enc_up, enc_down)
    terms, first_rows = lax.optimization_barrier((terms, first_rows))
    terms = terms + swap(terms, "section")
    terms, gains, w_query, w_key, w_value, w_out = lax.optimization_barrier(
        (terms, gains, w_query, w_key, w_value, w_out)
    )
    wq = lax.optimization_barrier(pair_gather(w_query, "section", 0))
    wk = lax.optimization_barrier(pair_gather(w_key, "section", 0))
    wv = lax.optimization_barrier(pair_gather(w_value, "section", 0))
    wo = lax.optimization_barrier(pair_gather(w_out, "section", 0))
    terms = terms.reshape(blocks_held, halves, half_rows, E)
    terms = pair_scatter_sum(terms, "mp", 1, jnp.bfloat16)
    terms = terms.reshape(blocks_held, half_rows, E)
    own_rows = lax.dynamic_slice_in_dim(database, mp_index * half_rows, half_rows, 1)
    enc_half = (own_rows.astype(jnp.float32) + terms).astype(jnp.bfloat16)

    id_table = neighbour_ids.reshape(db_count, request)
    owners = id_table // blocks_held
    within = id_table % blocks_held
    places = jnp.arange(request)
    same_owner = owners[:, :, None] == owners[:, None, :]
    earlier = places[None, None, :] < places[None, :, None]
    rank_in = jnp.sum((same_owner & earlier).astype(jnp.int32), axis=-1)
    single = jnp.sum(same_owner.astype(jnp.int32), axis=-1) == 1
    singles_before = jnp.sum((single[:, None, :] & earlier).astype(jnp.int32), axis=-1)
    channel = jnp.where(single, singles_before % channels, rank_in)
    same_channel = channel[:, :, None] == channel[:, None, :]
    slot_in = jnp.sum((same_channel & earlier).astype(jnp.int32), axis=-1)

    serve = (owners == db_index) & (channel == sec_index)
    send_local = jnp.sum(jnp.where(serve, within, 0), axis=-1)
    payload = enc_half[send_local]
    payload, first_rows = lax.optimization_barrier((payload, first_rows))
    queries = layer_queries(state, gains[0], wq[0], first_rows)
    received = lax.all_to_all(payload, "db", split_axis=0, concat_axis=0, tiled=True)
    received, queries, wk, wv, wo = lax.optimization_barrier((received, queries, wk, wv, wo))

    my_owner = lax.dynamic_index_in_dim(owners, db_index, 0, keepdims=False)
    my_channel = lax.dynamic_index_in_dim(channel, db_index, 0, keepdims=False)
    my_slot = lax.dynamic_index_in_dim(slot_in, db_index, 0, keepdims=False)
    pick = (my_channel[None, :] == sec_index) & (
        my_slot[None, :] == jnp.arange(per_channel)[:, None]
    )
    slot_owner = jnp.sum(jnp.where(pick, my_owner[None, :], 0), axis=-1)
    compact = received[slot_owner]
    channel_blocks = pair_gather(compact, "mp", 1)
    all_blocks = pair_gather(channel_blocks, "section", 0)
    flat_pos = my_channel * per_channel + my_slot
    mine = lax.dynamic_slice_in_dim(flat_pos, sec_index * per_channel, per_channel, 0)
    neighbours = all_blocks[mine]
    enc_blocks = neighbours.reshape(-1, NEIGH * NBLOCK, E)

    batches = 2
    batch_tokens = micro_tokens // batches
    batch_blocks = enc_blocks.shape[0] // batches
    states = [state[i * batch_tokens : (i + 1) * batch_tokens] for i in range(batches)]
    batch_queries = [queries[i * batch_tokens : (i + 1) * batch_tokens] for i in range(batches)]
    batch_neighbours = [
        enc_blocks[i * batch_blocks : (i + 1) * batch_blocks] for i in range(batches)
    ]
    for layer_id in range(wq.shape[0]):
        for i in range(batches):
            if layer_id > 0:
                batch_queries[i] = layer_queries(states[i], gains[layer_id], wq[layer_id])
            states[i] = cross_layer(
                states[i],
                batch_queries[i],
                batch_neighbours[i],
                wq[layer_id],
                wk[layer_id],
                wv[layer_id],
                wo[layer_id],
            )
    return jnp.concatenate(states, axis=0)


def solution(mesh):
    in_specs = (
        P("db", "mp"),
        P("db", None, None),
        P(),
        P(),
        P(None, ("section", "mp")),
        P(("section", "mp"), None),
        P("section", None),
        P("section", None, "mp"),
        P("section", None, "mp"),
        P("section", None, "mp"),
        P("section", "mp", None),
    )
    out_specs = P(("db", "section"), "mp")
    return jax.shard_map(body, mesh=mesh, in_specs=in_specs, out_specs=out_specs, check_vma=False)
```

```python
import jax
import jax.numpy as jnp
from jax import lax
from jax.sharding import PartitionSpec as P

HD = 128
E = 896
NEIGH = 2
QBLOCK = 64
NBLOCK = 128


def rms_scale(rows_in, gain_vec):
    return (
        rows_in * lax.rsqrt(jnp.mean(rows_in * rows_in, axis=-1, keepdims=True) + 1e-06) * gain_vec
    )


def encoder_terms(floats, enc_gain, enc_up, enc_down):
    normed = rms_scale(floats, enc_gain).astype(jnp.bfloat16)
    inner_act = jax.nn.gelu(
        jnp.dot(normed, enc_up, preferred_element_type=jnp.float32), approximate=True
    ).astype(jnp.bfloat16)
    return jnp.dot(inner_act, enc_down, preferred_element_type=jnp.float32)


def swap(block, axis):
    return lax.ppermute(block, axis, [(0, 1), (1, 0)])


def pair_gather(block, axis, dim):
    other = swap(block, axis)
    first = lax.axis_index(axis) == 0
    return jnp.where(
        first,
        jnp.concatenate([block, other], axis=dim),
        jnp.concatenate([other, block], axis=dim),
    )


def pair_scatter_sum(block, axis, dim, link_type):
    index = lax.axis_index(axis)
    half = block.shape[dim] // 2
    mine = lax.dynamic_slice_in_dim(block, index * half, half, dim)
    theirs = lax.dynamic_slice_in_dim(block, (1 - index) * half, half, dim)
    return mine + swap(theirs.astype(link_type), axis).astype(mine.dtype)


def layer_queries(state_rows, gain_vec, query_w, whole_rows=None):
    if whole_rows is None:
        whole_rows = pair_gather(state_rows, "mp", 1)
    floats = whole_rows.astype(jnp.float32)
    normed = rms_scale(floats, gain_vec).astype(jnp.bfloat16)
    return (jnp.dot(normed, query_w, preferred_element_type=jnp.float32) * HD ** (-0.5)).astype(
        jnp.bfloat16
    )


def cross_layer(state_rows, queries, blocks, query_w, key_w, value_w, out_w):
    block_count = blocks.shape[0]
    flat_rows = blocks.reshape(-1, E)
    key_rows = jnp.dot(flat_rows, key_w, preferred_element_type=jnp.float32).astype(jnp.bfloat16)
    value_rows = jnp.dot(flat_rows, value_w, preferred_element_type=jnp.float32).astype(
        jnp.bfloat16
    )
    head_count = query_w.shape[1] // HD
    query_four = queries.reshape(block_count, QBLOCK, head_count, HD)
    key_four = key_rows.reshape(block_count, NEIGH * NBLOCK, head_count, HD)
    value_four = value_rows.reshape(block_count, NEIGH * NBLOCK, head_count, HD)
    scores = jnp.einsum("cqhd,ckhd->chqk", query_four, key_four, preferred_element_type=jnp.float32)
    soft_weights = jax.nn.softmax(scores, axis=-1).astype(jnp.bfloat16)
    context = jnp.einsum(
        "chqk,ckhd->cqhd", soft_weights, value_four, preferred_element_type=jnp.float32
    )
    context = context.astype(jnp.bfloat16).reshape(block_count * QBLOCK, head_count * HD)
    partial_out = jnp.dot(context, out_w, preferred_element_type=jnp.float32)
    head_share = pair_scatter_sum(partial_out, "mp", 1, jnp.bfloat16)
    return (state_rows.astype(jnp.float32) + head_share).astype(jnp.bfloat16)


def body(
    hidden_in,
    database,
    neighbour_ids,
    enc_gain,
    enc_up,
    enc_down,
    dec_gain,
    w_query,
    w_key,
    w_value,
    w_out,
):
    db_count = lax.axis_size("db")
    db_index = lax.axis_index("db")
    channels = lax.axis_size("section")
    sec_index = lax.axis_index("section")
    halves = lax.axis_size("mp")
    mp_index = lax.axis_index("mp")
    blocks_held = database.shape[0]
    request = neighbour_ids.shape[0] // db_count * NEIGH
    per_channel = request // channels
    half_rows = NBLOCK // halves

    gains = pair_gather(dec_gain, "section", 0)
    micro_tokens = hidden_in.shape[0] // channels
    state = lax.dynamic_slice_in_dim(hidden_in, sec_index * micro_tokens, micro_tokens, 0)
    half_tokens = micro_tokens // 2
    rows_a = pair_gather(state[:half_tokens], "mp", 1)
    rows_b = pair_gather(state[half_tokens:], "mp", 1)

    held_rows = database.reshape(-1, E).astype(jnp.float32)
    terms = encoder_terms(held_rows, enc_gain, enc_up, enc_down)
    terms, rows_a = lax.optimization_barrier((terms, rows_a))
    terms = terms + swap(terms, "section")
    terms, gains, w_query, w_key, w_value, w_out = lax.optimization_barrier(
        (terms, gains, w_query, w_key, w_value, w_out)
    )
    wq = lax.optimization_barrier(pair_gather(w_query, "section", 0))
    wk = lax.optimization_barrier(pair_gather(w_key, "section", 0))
    wv = lax.optimization_barrier(pair_gather(w_value, "section", 0))
    wo = lax.optimization_barrier(pair_gather(w_out, "section", 0))
    terms, rows_b = lax.optimization_barrier((terms, rows_b))
    first_rows = jnp.concatenate([rows_a, rows_b], axis=0)
    terms = terms.reshape(blocks_held, halves, half_rows, E)
    terms = pair_scatter_sum(terms, "mp", 1, jnp.bfloat16)
    terms = terms.reshape(blocks_held, half_rows, E)
    own_rows = lax.dynamic_slice_in_dim(database, mp_index * half_rows, half_rows, 1)
    enc_half = (own_rows.astype(jnp.float32) + terms).astype(jnp.bfloat16)

    id_table = neighbour_ids.reshape(db_count, request)
    owners = id_table // blocks_held
    within = id_table % blocks_held
    places = jnp.arange(request)
    same_owner = owners[:, :, None] == owners[:, None, :]
    earlier = places[None, None, :] < places[None, :, None]
    rank_in = jnp.sum((same_owner & earlier).astype(jnp.int32), axis=-1)
    single = jnp.sum(same_owner.astype(jnp.int32), axis=-1) == 1
    singles_before = jnp.sum((single[:, None, :] & earlier).astype(jnp.int32), axis=-1)
    channel = jnp.where(single, singles_before % channels, rank_in)
    same_channel = channel[:, :, None] == channel[:, None, :]
    slot_in = jnp.sum((same_channel & earlier).astype(jnp.int32), axis=-1)

    serve = (owners == db_index) & (channel == sec_index)
    send_local = jnp.sum(jnp.where(serve, within, 0), axis=-1)
    payload = enc_half[send_local]
    payload, first_rows = lax.optimization_barrier((payload, first_rows))
    queries = layer_queries(state, gains[0], wq[0], first_rows)
    received = lax.all_to_all(payload, "db", split_axis=0, concat_axis=0, tiled=True)
    received, queries, wk, wv, wo = lax.optimization_barrier((received, queries, wk, wv, wo))

    my_owner = lax.dynamic_index_in_dim(owners, db_index, 0, keepdims=False)
    my_channel = lax.dynamic_index_in_dim(channel, db_index, 0, keepdims=False)
    my_slot = lax.dynamic_index_in_dim(slot_in, db_index, 0, keepdims=False)
    pick = (my_channel[None, :] == sec_index) & (
        my_slot[None, :] == jnp.arange(per_channel)[:, None]
    )
    slot_owner = jnp.sum(jnp.where(pick, my_owner[None, :], 0), axis=-1)
    compact = received[slot_owner]
    channel_blocks = pair_gather(compact, "mp", 1)
    all_blocks = pair_gather(channel_blocks, "section", 0)
    flat_pos = my_channel * per_channel + my_slot
    mine = lax.dynamic_slice_in_dim(flat_pos, sec_index * per_channel, per_channel, 0)
    neighbours = all_blocks[mine]
    enc_blocks = neighbours.reshape(-1, NEIGH * NBLOCK, E)

    batches = 2
    batch_tokens = micro_tokens // batches
    batch_blocks = enc_blocks.shape[0] // batches
    states = [state[i * batch_tokens : (i + 1) * batch_tokens] for i in range(batches)]
    batch_queries = [queries[i * batch_tokens : (i + 1) * batch_tokens] for i in range(batches)]
    batch_neighbours = [
        enc_blocks[i * batch_blocks : (i + 1) * batch_blocks] for i in range(batches)
    ]
    for layer_id in range(wq.shape[0]):
        for i in range(batches):
            if layer_id > 0:
                batch_queries[i] = layer_queries(states[i], gains[layer_id], wq[layer_id])
            states[i] = cross_layer(
                states[i],
                batch_queries[i],
                batch_neighbours[i],
                wq[layer_id],
                wk[layer_id],
                wv[layer_id],
                wo[layer_id],
            )
    return jnp.concatenate(states, axis=0)


def solution(mesh):
    in_specs = (
        P("db", "mp"),
        P("db", None, None),
        P(),
        P(),
        P(None, ("section", "mp")),
        P(("section", "mp"), None),
        P("section", None),
        P("section", None, "mp"),
        P("section", None, "mp"),
        P("section", None, "mp"),
        P("section", "mp", None),
    )
    out_specs = P(("db", "section"), "mp")
    return jax.shard_map(body, mesh=mesh, in_specs=in_specs, out_specs=out_specs, check_vma=False)
```

```python
import jax
import jax.numpy as jnp
from jax import lax
from jax.sharding import PartitionSpec as P

HD = 128
E = 896
NEIGH = 2
QBLOCK = 64
NBLOCK = 128


def rms_scale(rows_in, gain_vec):
    return (
        rows_in * lax.rsqrt(jnp.mean(rows_in * rows_in, axis=-1, keepdims=True) + 1e-06) * gain_vec
    )


def encoder_terms(floats, enc_gain, enc_up, enc_down):
    normed = rms_scale(floats, enc_gain).astype(jnp.bfloat16)
    inner_act = jax.nn.gelu(
        jnp.dot(normed, enc_up, preferred_element_type=jnp.float32), approximate=True
    ).astype(jnp.bfloat16)
    return jnp.dot(inner_act, enc_down, preferred_element_type=jnp.float32)


def swap(block, axis):
    return lax.ppermute(block, axis, [(0, 1), (1, 0)])


def pair_gather(block, axis, dim):
    other = swap(block, axis)
    first = lax.axis_index(axis) == 0
    return jnp.where(
        first,
        jnp.concatenate([block, other], axis=dim),
        jnp.concatenate([other, block], axis=dim),
    )


def pair_scatter_sum(block, axis, dim, link_type):
    index = lax.axis_index(axis)
    half = block.shape[dim] // 2
    mine = lax.dynamic_slice_in_dim(block, index * half, half, dim)
    theirs = lax.dynamic_slice_in_dim(block, (1 - index) * half, half, dim)
    return mine + swap(theirs.astype(link_type), axis).astype(mine.dtype)


def layer_queries(state_rows, gain_vec, query_w, whole_rows=None):
    if whole_rows is None:
        whole_rows = pair_gather(state_rows, "mp", 1)
    floats = whole_rows.astype(jnp.float32)
    normed = rms_scale(floats, gain_vec).astype(jnp.bfloat16)
    return (jnp.dot(normed, query_w, preferred_element_type=jnp.float32) * HD ** (-0.5)).astype(
        jnp.bfloat16
    )


def cross_layer(state_rows, queries, blocks, query_w, key_w, value_w, out_w):
    block_count = blocks.shape[0]
    flat_rows = blocks.reshape(-1, E)
    key_rows = jnp.dot(flat_rows, key_w, preferred_element_type=jnp.float32).astype(jnp.bfloat16)
    value_rows = jnp.dot(flat_rows, value_w, preferred_element_type=jnp.float32).astype(
        jnp.bfloat16
    )
    head_count = query_w.shape[1] // HD
    query_four = queries.reshape(block_count, QBLOCK, head_count, HD)
    key_four = key_rows.reshape(block_count, NEIGH * NBLOCK, head_count, HD)
    value_four = value_rows.reshape(block_count, NEIGH * NBLOCK, head_count, HD)
    scores = jnp.einsum("cqhd,ckhd->chqk", query_four, key_four, preferred_element_type=jnp.float32)
    soft_weights = jax.nn.softmax(scores, axis=-1).astype(jnp.bfloat16)
    context = jnp.einsum(
        "chqk,ckhd->cqhd", soft_weights, value_four, preferred_element_type=jnp.float32
    )
    context = context.astype(jnp.bfloat16).reshape(block_count * QBLOCK, head_count * HD)
    partial_out = jnp.dot(context, out_w, preferred_element_type=jnp.float32)
    head_share = pair_scatter_sum(partial_out, "mp", 1, jnp.bfloat16)
    return (state_rows.astype(jnp.float32) + head_share).astype(jnp.bfloat16)


def body(
    hidden_in,
    database,
    neighbour_ids,
    enc_gain,
    enc_up,
    enc_down,
    dec_gain,
    w_query,
    w_key,
    w_value,
    w_out,
):
    db_count = lax.axis_size("db")
    db_index = lax.axis_index("db")
    channels = lax.axis_size("section")
    sec_index = lax.axis_index("section")
    halves = lax.axis_size("mp")
    mp_index = lax.axis_index("mp")
    blocks_held = database.shape[0]
    request = neighbour_ids.shape[0] // db_count * NEIGH
    per_channel = request // channels
    half_rows = NBLOCK // halves

    gains = pair_gather(dec_gain, "section", 0)
    micro_tokens = hidden_in.shape[0] // channels
    state = lax.dynamic_slice_in_dim(hidden_in, sec_index * micro_tokens, micro_tokens, 0)
    half_tokens = micro_tokens // 2
    rows_a = pair_gather(state[:half_tokens], "mp", 1)
    rows_b = pair_gather(state[half_tokens:], "mp", 1)

    held_rows = database.reshape(-1, E).astype(jnp.float32)
    terms = encoder_terms(held_rows, enc_gain, enc_up, enc_down)
    terms, rows_a = lax.optimization_barrier((terms, rows_a))
    sibling_terms = swap(terms, "section")
    sibling_terms, rows_b = lax.optimization_barrier((sibling_terms, rows_b))
    terms = terms + sibling_terms
    terms, gains, w_query, w_key, w_value, w_out = lax.optimization_barrier(
        (terms, gains, w_query, w_key, w_value, w_out)
    )
    wq = lax.optimization_barrier(pair_gather(w_query, "section", 0))
    wk = lax.optimization_barrier(pair_gather(w_key, "section", 0))
    wv = lax.optimization_barrier(pair_gather(w_value, "section", 0))
    wo = lax.optimization_barrier(pair_gather(w_out, "section", 0))
    first_rows = jnp.concatenate([rows_a, rows_b], axis=0)
    terms = terms.reshape(blocks_held, halves, half_rows, E)
    terms = pair_scatter_sum(terms, "mp", 1, jnp.bfloat16)
    terms = terms.reshape(blocks_held, half_rows, E)
    own_rows = lax.dynamic_slice_in_dim(database, mp_index * half_rows, half_rows, 1)
    enc_half = (own_rows.astype(jnp.float32) + terms).astype(jnp.bfloat16)

    id_table = neighbour_ids.reshape(db_count, request)
    owners = id_table // blocks_held
    within = id_table % blocks_held
    places = jnp.arange(request)
    same_owner = owners[:, :, None] == owners[:, None, :]
    earlier = places[None, None, :] < places[None, :, None]
    rank_in = jnp.sum((same_owner & earlier).astype(jnp.int32), axis=-1)
    single = jnp.sum(same_owner.astype(jnp.int32), axis=-1) == 1
    singles_before = jnp.sum((single[:, None, :] & earlier).astype(jnp.int32), axis=-1)
    channel = jnp.where(single, singles_before % channels, rank_in)
    same_channel = channel[:, :, None] == channel[:, None, :]
    slot_in = jnp.sum((same_channel & earlier).astype(jnp.int32), axis=-1)

    serve = (owners == db_index) & (channel == sec_index)
    send_local = jnp.sum(jnp.where(serve, within, 0), axis=-1)
    payload = enc_half[send_local]
    payload, first_rows = lax.optimization_barrier((payload, first_rows))
    queries = layer_queries(state, gains[0], wq[0], first_rows)
    received = lax.all_to_all(payload, "db", split_axis=0, concat_axis=0, tiled=True)
    received, queries, wk, wv, wo = lax.optimization_barrier((received, queries, wk, wv, wo))

    my_owner = lax.dynamic_index_in_dim(owners, db_index, 0, keepdims=False)
    my_channel = lax.dynamic_index_in_dim(channel, db_index, 0, keepdims=False)
    my_slot = lax.dynamic_index_in_dim(slot_in, db_index, 0, keepdims=False)
    pick = (my_channel[None, :] == sec_index) & (
        my_slot[None, :] == jnp.arange(per_channel)[:, None]
    )
    slot_owner = jnp.sum(jnp.where(pick, my_owner[None, :], 0), axis=-1)
    compact = received[slot_owner]
    channel_blocks = pair_gather(compact, "mp", 1)
    all_blocks = pair_gather(channel_blocks, "section", 0)
    flat_pos = my_channel * per_channel + my_slot
    mine = lax.dynamic_slice_in_dim(flat_pos, sec_index * per_channel, per_channel, 0)
    neighbours = all_blocks[mine]
    enc_blocks = neighbours.reshape(-1, NEIGH * NBLOCK, E)

    batches = 2
    batch_tokens = micro_tokens // batches
    batch_blocks = enc_blocks.shape[0] // batches
    states = [state[i * batch_tokens : (i + 1) * batch_tokens] for i in range(batches)]
    batch_queries = [queries[i * batch_tokens : (i + 1) * batch_tokens] for i in range(batches)]
    batch_neighbours = [
        enc_blocks[i * batch_blocks : (i + 1) * batch_blocks] for i in range(batches)
    ]
    for layer_id in range(wq.shape[0]):
        for i in range(batches):
            if layer_id > 0:
                batch_queries[i] = layer_queries(states[i], gains[layer_id], wq[layer_id])
            states[i] = cross_layer(
                states[i],
                batch_queries[i],
                batch_neighbours[i],
                wq[layer_id],
                wk[layer_id],
                wv[layer_id],
                wo[layer_id],
            )
    return jnp.concatenate(states, axis=0)


def solution(mesh):
    in_specs = (
        P("db", "mp"),
        P("db", None, None),
        P(),
        P(),
        P(None, ("section", "mp")),
        P(("section", "mp"), None),
        P("section", None),
        P("section", None, "mp"),
        P("section", None, "mp"),
        P("section", None, "mp"),
        P("section", "mp", None),
    )
    out_specs = P(("db", "section"), "mp")
    return jax.shard_map(body, mesh=mesh, in_specs=in_specs, out_specs=out_specs, check_vma=False)
```

```python
import jax
import jax.numpy as jnp
from jax import lax
from jax.sharding import PartitionSpec as P

HD = 128
E = 896
NEIGH = 2
QBLOCK = 64
NBLOCK = 128


def rms_scale(rows_in, gain_vec):
    return (
        rows_in * lax.rsqrt(jnp.mean(rows_in * rows_in, axis=-1, keepdims=True) + 1e-06) * gain_vec
    )


def encoder_terms(floats, enc_gain, enc_up, enc_down):
    normed = rms_scale(floats, enc_gain).astype(jnp.bfloat16)
    inner_act = jax.nn.gelu(
        jnp.dot(normed, enc_up, preferred_element_type=jnp.float32), approximate=True
    ).astype(jnp.bfloat16)
    return jnp.dot(inner_act, enc_down, preferred_element_type=jnp.float32)


def swap(block, axis):
    return lax.ppermute(block, axis, [(0, 1), (1, 0)])


def pair_gather(block, axis, dim):
    other = swap(block, axis)
    first = lax.axis_index(axis) == 0
    return jnp.where(
        first,
        jnp.concatenate([block, other], axis=dim),
        jnp.concatenate([other, block], axis=dim),
    )


def pair_scatter_sum(block, axis, dim, link_type):
    index = lax.axis_index(axis)
    half = block.shape[dim] // 2
    mine = lax.dynamic_slice_in_dim(block, index * half, half, dim)
    theirs = lax.dynamic_slice_in_dim(block, (1 - index) * half, half, dim)
    return mine + swap(theirs.astype(link_type), axis).astype(mine.dtype)


def layer_queries(state_rows, gain_vec, query_w, whole_rows=None):
    if whole_rows is None:
        whole_rows = pair_gather(state_rows, "mp", 1)
    floats = whole_rows.astype(jnp.float32)
    normed = rms_scale(floats, gain_vec).astype(jnp.bfloat16)
    return (jnp.dot(normed, query_w, preferred_element_type=jnp.float32) * HD ** (-0.5)).astype(
        jnp.bfloat16
    )


def cross_layer(state_rows, queries, blocks, query_w, key_w, value_w, out_w):
    block_count = blocks.shape[0]
    flat_rows = blocks.reshape(-1, E)
    key_rows = jnp.dot(flat_rows, key_w, preferred_element_type=jnp.float32).astype(jnp.bfloat16)
    value_rows = jnp.dot(flat_rows, value_w, preferred_element_type=jnp.float32).astype(
        jnp.bfloat16
    )
    head_count = query_w.shape[1] // HD
    query_four = queries.reshape(block_count, QBLOCK, head_count, HD)
    key_four = key_rows.reshape(block_count, NEIGH * NBLOCK, head_count, HD)
    value_four = value_rows.reshape(block_count, NEIGH * NBLOCK, head_count, HD)
    scores = jnp.einsum("cqhd,ckhd->chqk", query_four, key_four, preferred_element_type=jnp.float32)
    soft_weights = jax.nn.softmax(scores, axis=-1).astype(jnp.bfloat16)
    context = jnp.einsum(
        "chqk,ckhd->cqhd", soft_weights, value_four, preferred_element_type=jnp.float32
    )
    context = context.astype(jnp.bfloat16).reshape(block_count * QBLOCK, head_count * HD)
    partial_out = jnp.dot(context, out_w, preferred_element_type=jnp.float32)
    head_share = pair_scatter_sum(partial_out, "mp", 1, jnp.bfloat16)
    return (state_rows.astype(jnp.float32) + head_share).astype(jnp.bfloat16)


def body(
    hidden_in,
    database,
    neighbour_ids,
    enc_gain,
    enc_up,
    enc_down,
    dec_gain,
    w_query,
    w_key,
    w_value,
    w_out,
):
    db_count = lax.axis_size("db")
    db_index = lax.axis_index("db")
    channels = lax.axis_size("section")
    sec_index = lax.axis_index("section")
    halves = lax.axis_size("mp")
    mp_index = lax.axis_index("mp")
    blocks_held = database.shape[0]
    request = neighbour_ids.shape[0] // db_count * NEIGH
    per_channel = request // channels
    half_rows = NBLOCK // halves

    gains = pair_gather(dec_gain, "section", 0)
    micro_tokens = hidden_in.shape[0] // channels
    state = lax.dynamic_slice_in_dim(hidden_in, sec_index * micro_tokens, micro_tokens, 0)
    half_tokens = micro_tokens // 2
    rows_a = pair_gather(state[:half_tokens], "mp", 1)
    rows_b = pair_gather(state[half_tokens:], "mp", 1)

    held_rows = database.reshape(-1, E).astype(jnp.float32)
    terms = encoder_terms(held_rows, enc_gain, enc_up, enc_down)
    terms, rows_a = lax.optimization_barrier((terms, rows_a))
    terms = terms + swap(terms, "section")
    terms, gains, w_query, w_key, w_value, w_out = lax.optimization_barrier(
        (terms, gains, w_query, w_key, w_value, w_out)
    )
    wq = lax.optimization_barrier(pair_gather(w_query, "section", 0))
    wk = lax.optimization_barrier(pair_gather(w_key, "section", 0))
    wv = lax.optimization_barrier(pair_gather(w_value, "section", 0))
    wo = lax.optimization_barrier(pair_gather(w_out, "section", 0))
    terms, rows_b = lax.optimization_barrier((terms, rows_b))
    first_rows = jnp.concatenate([rows_a, rows_b], axis=0)
    terms = terms.reshape(blocks_held, halves, half_rows, E)
    terms = pair_scatter_sum(terms, "mp", 1, jnp.bfloat16)
    terms = terms.reshape(blocks_held, half_rows, E)
    own_rows = lax.dynamic_slice_in_dim(database, mp_index * half_rows, half_rows, 1)
    enc_half = (own_rows.astype(jnp.float32) + terms).astype(jnp.bfloat16)

    id_table = neighbour_ids.reshape(db_count, request)
    owners = id_table // blocks_held
    within = id_table % blocks_held
    places = jnp.arange(request)
    same_owner = owners[:, :, None] == owners[:, None, :]
    earlier = places[None, None, :] < places[None, :, None]
    rank_in = jnp.sum((same_owner & earlier).astype(jnp.int32), axis=-1)
    single = jnp.sum(same_owner.astype(jnp.int32), axis=-1) == 1
    singles_before = jnp.sum((single[:, None, :] & earlier).astype(jnp.int32), axis=-1)
    channel = jnp.where(single, singles_before % channels, rank_in)
    same_channel = channel[:, :, None] == channel[:, None, :]
    slot_in = jnp.sum((same_channel & earlier).astype(jnp.int32), axis=-1)

    serve = (owners == db_index) & (channel == sec_index)
    send_local = jnp.sum(jnp.where(serve, within, 0), axis=-1)
    payload = enc_half[send_local]
    payload, first_rows = lax.optimization_barrier((payload, first_rows))
    queries = layer_queries(state, gains[0], wq[0], first_rows)
    received = lax.all_to_all(payload, "db", split_axis=0, concat_axis=0, tiled=True)
    received, queries, wk, wv, wo = lax.optimization_barrier((received, queries, wk, wv, wo))

    my_owner = lax.dynamic_index_in_dim(owners, db_index, 0, keepdims=False)
    my_channel = lax.dynamic_index_in_dim(channel, db_index, 0, keepdims=False)
    my_slot = lax.dynamic_index_in_dim(slot_in, db_index, 0, keepdims=False)
    pick = (my_channel[None, :] == sec_index) & (
        my_slot[None, :] == jnp.arange(per_channel)[:, None]
    )
    slot_owner = jnp.sum(jnp.where(pick, my_owner[None, :], 0), axis=-1)
    compact = received[slot_owner]
    channel_blocks = pair_gather(compact, "mp", 1)
    sibling_blocks = swap(channel_blocks, "section")
    mine_channel = lax.dynamic_slice_in_dim(my_channel, sec_index * per_channel, per_channel, 0)
    mine_slot = lax.dynamic_slice_in_dim(my_slot, sec_index * per_channel, per_channel, 0)
    neighbours = jnp.where(
        (mine_channel == sec_index)[:, None, None],
        channel_blocks[mine_slot],
        sibling_blocks[mine_slot],
    )
    enc_blocks = neighbours.reshape(-1, NEIGH * NBLOCK, E)

    batches = 2
    batch_tokens = micro_tokens // batches
    batch_blocks = enc_blocks.shape[0] // batches
    states = [state[i * batch_tokens : (i + 1) * batch_tokens] for i in range(batches)]
    batch_queries = [queries[i * batch_tokens : (i + 1) * batch_tokens] for i in range(batches)]
    batch_neighbours = [
        enc_blocks[i * batch_blocks : (i + 1) * batch_blocks] for i in range(batches)
    ]
    for layer_id in range(wq.shape[0]):
        for i in range(batches):
            if layer_id > 0:
                batch_queries[i] = layer_queries(states[i], gains[layer_id], wq[layer_id])
            states[i] = cross_layer(
                states[i],
                batch_queries[i],
                batch_neighbours[i],
                wq[layer_id],
                wk[layer_id],
                wv[layer_id],
                wo[layer_id],
            )
    return jnp.concatenate(states, axis=0)


def solution(mesh):
    in_specs = (
        P("db", "mp"),
        P("db", None, None),
        P(),
        P(),
        P(None, ("section", "mp")),
        P(("section", "mp"), None),
        P("section", None),
        P("section", None, "mp"),
        P("section", None, "mp"),
        P("section", None, "mp"),
        P("section", "mp", None),
    )
    out_specs = P(("db", "section"), "mp")
    return jax.shard_map(body, mesh=mesh, in_specs=in_specs, out_specs=out_specs, check_vma=False)
```

```python
import jax
import jax.numpy as jnp
from jax import lax
from jax.sharding import PartitionSpec as P

HD = 128
E = 896
NEIGH = 2
QBLOCK = 64
NBLOCK = 128


def rms_scale(rows_in, gain_vec):
    return (
        rows_in * lax.rsqrt(jnp.mean(rows_in * rows_in, axis=-1, keepdims=True) + 1e-06) * gain_vec
    )


def encoder_terms(floats, enc_gain, enc_up, enc_down):
    normed = rms_scale(floats, enc_gain).astype(jnp.bfloat16)
    inner_act = jax.nn.gelu(
        jnp.dot(normed, enc_up, preferred_element_type=jnp.float32), approximate=True
    ).astype(jnp.bfloat16)
    return jnp.dot(inner_act, enc_down, preferred_element_type=jnp.float32)


def swap(block, axis):
    return lax.ppermute(block, axis, [(0, 1), (1, 0)])


def pair_gather(block, axis, dim):
    other = swap(block, axis)
    first = lax.axis_index(axis) == 0
    return jnp.where(
        first,
        jnp.concatenate([block, other], axis=dim),
        jnp.concatenate([other, block], axis=dim),
    )


def pair_scatter_sum(block, axis, dim, link_type):
    index = lax.axis_index(axis)
    half = block.shape[dim] // 2
    mine = lax.dynamic_slice_in_dim(block, index * half, half, dim)
    theirs = lax.dynamic_slice_in_dim(block, (1 - index) * half, half, dim)
    return mine + swap(theirs.astype(link_type), axis).astype(mine.dtype)


def layer_queries(state_rows, gain_vec, query_w, whole_rows=None):
    if whole_rows is None:
        whole_rows = pair_gather(state_rows, "mp", 1)
    floats = whole_rows.astype(jnp.float32)
    normed = rms_scale(floats, gain_vec).astype(jnp.bfloat16)
    return (jnp.dot(normed, query_w, preferred_element_type=jnp.float32) * HD ** (-0.5)).astype(
        jnp.bfloat16
    )


def cross_layer(state_rows, queries, blocks, query_w, key_w, value_w, out_w):
    block_count = blocks.shape[0]
    key_rows, value_rows = key_w, value_w
    head_count = query_w.shape[1] // HD
    query_four = queries.reshape(block_count, QBLOCK, head_count, HD)
    key_four = key_rows.reshape(block_count, NEIGH * NBLOCK, head_count, HD)
    value_four = value_rows.reshape(block_count, NEIGH * NBLOCK, head_count, HD)
    scores = jnp.einsum("cqhd,ckhd->chqk", query_four, key_four, preferred_element_type=jnp.float32)
    soft_weights = jax.nn.softmax(scores, axis=-1).astype(jnp.bfloat16)
    context = jnp.einsum(
        "chqk,ckhd->cqhd", soft_weights, value_four, preferred_element_type=jnp.float32
    )
    context = context.astype(jnp.bfloat16).reshape(block_count * QBLOCK, head_count * HD)
    partial_out = jnp.dot(context, out_w, preferred_element_type=jnp.float32)
    head_share = pair_scatter_sum(partial_out, "mp", 1, jnp.bfloat16)
    return (state_rows.astype(jnp.float32) + head_share).astype(jnp.bfloat16)


def body(
    hidden_in,
    database,
    neighbour_ids,
    enc_gain,
    enc_up,
    enc_down,
    dec_gain,
    w_query,
    w_key,
    w_value,
    w_out,
):
    db_count = lax.axis_size("db")
    db_index = lax.axis_index("db")
    channels = lax.axis_size("section")
    sec_index = lax.axis_index("section")
    halves = lax.axis_size("mp")
    mp_index = lax.axis_index("mp")
    blocks_held = database.shape[0]
    request = neighbour_ids.shape[0] // db_count * NEIGH
    per_channel = request // channels
    half_rows = NBLOCK // halves

    gains = pair_gather(dec_gain, "section", 0)
    micro_tokens = hidden_in.shape[0] // channels
    state = lax.dynamic_slice_in_dim(hidden_in, sec_index * micro_tokens, micro_tokens, 0)
    half_tokens = micro_tokens // 2
    rows_a = pair_gather(state[:half_tokens], "mp", 1)
    rows_b = pair_gather(state[half_tokens:], "mp", 1)

    held_rows = database.reshape(-1, E).astype(jnp.float32)
    terms = encoder_terms(held_rows, enc_gain, enc_up, enc_down)
    terms, rows_a = lax.optimization_barrier((terms, rows_a))
    terms = terms + swap(terms, "section")
    terms, gains, w_query, w_key, w_value, w_out = lax.optimization_barrier(
        (terms, gains, w_query, w_key, w_value, w_out)
    )
    wq = lax.optimization_barrier(pair_gather(w_query, "section", 0))
    wk = lax.optimization_barrier(pair_gather(w_key, "section", 0))
    wv = lax.optimization_barrier(pair_gather(w_value, "section", 0))
    wo = lax.optimization_barrier(pair_gather(w_out, "section", 0))
    terms, rows_b = lax.optimization_barrier((terms, rows_b))
    first_rows = jnp.concatenate([rows_a, rows_b], axis=0)
    terms = terms.reshape(blocks_held, halves, half_rows, E)
    terms = pair_scatter_sum(terms, "mp", 1, jnp.bfloat16)
    terms = terms.reshape(blocks_held, half_rows, E)
    own_rows = lax.dynamic_slice_in_dim(database, mp_index * half_rows, half_rows, 1)
    enc_half = (own_rows.astype(jnp.float32) + terms).astype(jnp.bfloat16)

    id_table = neighbour_ids.reshape(db_count, request)
    owners = id_table // blocks_held
    within = id_table % blocks_held
    places = jnp.arange(request)
    same_owner = owners[:, :, None] == owners[:, None, :]
    earlier = places[None, None, :] < places[None, :, None]
    rank_in = jnp.sum((same_owner & earlier).astype(jnp.int32), axis=-1)
    single = jnp.sum(same_owner.astype(jnp.int32), axis=-1) == 1
    singles_before = jnp.sum((single[:, None, :] & earlier).astype(jnp.int32), axis=-1)
    channel = jnp.where(single, singles_before % channels, rank_in)
    same_channel = channel[:, :, None] == channel[:, None, :]
    slot_in = jnp.sum((same_channel & earlier).astype(jnp.int32), axis=-1)

    serve = (owners == db_index) & (channel == sec_index)
    send_local = jnp.sum(jnp.where(serve, within, 0), axis=-1)
    payload = enc_half[send_local]
    payload, first_rows = lax.optimization_barrier((payload, first_rows))
    queries = layer_queries(state, gains[0], wq[0], first_rows)
    received = lax.all_to_all(payload, "db", split_axis=0, concat_axis=0, tiled=True)
    received, queries, wk, wv, wo = lax.optimization_barrier((received, queries, wk, wv, wo))

    my_owner = lax.dynamic_index_in_dim(owners, db_index, 0, keepdims=False)
    my_channel = lax.dynamic_index_in_dim(channel, db_index, 0, keepdims=False)
    my_slot = lax.dynamic_index_in_dim(slot_in, db_index, 0, keepdims=False)
    pick = (my_channel[None, :] == sec_index) & (
        my_slot[None, :] == jnp.arange(per_channel)[:, None]
    )
    slot_owner = jnp.sum(jnp.where(pick, my_owner[None, :], 0), axis=-1)
    compact = received[slot_owner]
    channel_blocks = pair_gather(compact, "mp", 1)
    all_blocks = pair_gather(channel_blocks, "section", 0)
    flat_pos = my_channel * per_channel + my_slot
    mine = lax.dynamic_slice_in_dim(flat_pos, sec_index * per_channel, per_channel, 0)
    neighbours = all_blocks[mine]
    enc_blocks = neighbours.reshape(-1, NEIGH * NBLOCK, E)

    batches = 2
    batch_tokens = micro_tokens // batches
    batch_blocks = enc_blocks.shape[0] // batches
    states = [state[i * batch_tokens : (i + 1) * batch_tokens] for i in range(batches)]
    batch_queries = [queries[i * batch_tokens : (i + 1) * batch_tokens] for i in range(batches)]
    batch_neighbours = [
        enc_blocks[i * batch_blocks : (i + 1) * batch_blocks] for i in range(batches)
    ]
    flat_rows = enc_blocks.reshape(-1, E)
    batch_rows = batch_blocks * NEIGH * NBLOCK
    for layer_id in range(wq.shape[0]):
        key_all = jnp.dot(flat_rows, wk[layer_id], preferred_element_type=jnp.float32).astype(
            jnp.bfloat16
        )
        value_all = jnp.dot(flat_rows, wv[layer_id], preferred_element_type=jnp.float32).astype(
            jnp.bfloat16
        )
        for i in range(batches):
            if layer_id > 0:
                batch_queries[i] = layer_queries(states[i], gains[layer_id], wq[layer_id])
            states[i] = cross_layer(
                states[i],
                batch_queries[i],
                batch_neighbours[i],
                wq[layer_id],
                key_all[i * batch_rows : (i + 1) * batch_rows],
                value_all[i * batch_rows : (i + 1) * batch_rows],
                wo[layer_id],
            )
    return jnp.concatenate(states, axis=0)


def solution(mesh):
    in_specs = (
        P("db", "mp"),
        P("db", None, None),
        P(),
        P(),
        P(None, ("section", "mp")),
        P(("section", "mp"), None),
        P("section", None),
        P("section", None, "mp"),
        P("section", None, "mp"),
        P("section", None, "mp"),
        P("section", "mp", None),
    )
    out_specs = P(("db", "section"), "mp")
    return jax.shard_map(body, mesh=mesh, in_specs=in_specs, out_specs=out_specs, check_vma=False)
```
